128 devices in a mesh: slab: 8 (over y, core), tile: 16 (over z, x).
Axes of the slice: x: 4, y: 4, z: 4, core: 2. Of those that a mesh axis runs over, the one named last changes fastest.
Arguments:
- positions: float32 [3, 262144], P(None, ('slab', 'tile')), may hold values from -6 to 6
- radius: float32 [262144], P(('slab', 'tile')), may hold values from 0.7 to 1.4
- uptake_rate: float32 [262144], P(('slab', 'tile')), may hold values from 0.3 to 3
- voxel_local: int32 [262144], P(('slab', 'tile')), may hold values from 0 to 262143
- cell_counts: int32 [128], P(('slab', 'tile')), may hold values from 512 to 2048, as said below
- send_counts: int32 [128, 16], P(('slab', 'tile')), may hold values from 0 to 256, as said below
- neighbor_blocks: int32 [2048, 8], P(('slab', 'tile')), may hold values from 0 to 23, as said below
- field: float32 [2, 64, 256, 2048], P(None, 'slab', 'tile'), may hold values from 0.2 to 2
Outputs:
- velocity: float32 [3, 262144], P(None, ('slab', 'tile'))
- field_next: float32 [2, 64, 256, 2048], P(None, 'slab', 'tile')
The draws below stay inside these ranges and needn't reach their ends.
Inputs may be any that keep to these rules, and one draw needn't show every extreme that they name: `cell_counts`: A multiple of 128; in every slab one tile holds 2048 live cells and another 2048 // 4. `send_counts`: row g sums to cell_counts[g]; in every slab all tiles send exactly 256 cells to one common destination tile. `neighbor_blocks`: row g * 16 + b names 8 different blocks of tile g's extended table, the first being 4 + b.
All inputs are finite; a program needn't handle non-finite values.
Results may differ from the reference program's by a relative error of at most 0.0003.
Values sent between devices are 32-bit elements; how exact they have to be, the bound alone decides.
No kernel may reach another device: no remote copies, remote signals or barrier semaphores. Data moves between devices by JAX's collectives and lax.ppermute only.
A program may use at most 64 MiB of HBM per device.

```python
import math
import jax
import jax.numpy as jnp
from jax import lax

CZ = 8
CY = 16
NX = 2048
CAP = 2048
HB = 4
K = 8
ITERS = 4
NB = 16
SLOT = 256
NZ = 64
NY = 256
CELLS = 262144
N_SLAB = 8
N_TILE = 16


def count_tables(key):
    base = jax.random.fold_in(key, 7)
    keys = jax.random.split(base, 4)
    quarter = NB // 4
    blocks = jax.random.randint(keys[0], (N_SLAB, N_TILE), quarter, NB + 1)
    full_at = jax.random.randint(keys[1], (N_SLAB, 1), 0, N_TILE)
    low_at = (full_at + 1 + jax.random.randint(keys[2], (N_SLAB, 1), 0, N_TILE - 1)) % N_TILE
    lanes = jnp.arange(N_TILE, dtype=jnp.int32)[None, :]
    blocks = jnp.where(lanes == full_at, NB, jnp.where(lanes == low_at, quarter, blocks))
    living = (blocks * 128).reshape(-1).astype(jnp.int32)
    rows = N_SLAB * N_TILE
    others = N_TILE - 1
    remain = living - SLOT
    even_share = remain // others
    extra = remain % others
    places = jnp.arange(others, dtype=jnp.int32)[None, :]
    shares = even_share[:, None] + (places < extra[:, None]).astype(jnp.int32)
    reach = even_share // 2
    noise = jax.random.randint(keys[3], (rows, others), 0, 1 << 20)
    wobble = noise % (2 * reach[:, None] + 1) - reach[:, None]
    paired = (places % 2 == 0) & (places + 1 < others)
    wobble = jnp.where(paired, wobble, 0)
    shares = shares + wobble - jnp.roll(wobble, 1, axis=1)
    target = jnp.repeat(full_at, N_TILE, axis=0)
    zeros_col = jnp.zeros((rows, 1), jnp.int32)
    before = jnp.concatenate([shares, zeros_col], axis=1)
    after = jnp.concatenate([zeros_col, shares], axis=1)
    sends = jnp.where(lanes < target, before, jnp.where(lanes == target, SLOT, after))
    return (living, sends.astype(jnp.int32))


def draw_cell_counts(key, part):
    return count_tables(key)[0]


def draw_send_counts(key, part):
    return count_tables(key)[1]


def draw_neighbor_blocks(key, part):
    rows = N_SLAB * N_TILE * NB
    span = NB + 2 * HB
    keys = jax.random.split(jax.random.fold_in(key, 11), rows)
    own = (HB + jnp.arange(rows, dtype=jnp.int32) % NB).astype(jnp.int32)

    def choose(single, itself):
        order = jax.random.permutation(single, span - 1)[:K - 1].astype(jnp.int32)
        order = jnp.where(order >= itself, order + 1, order)
        return jnp.concatenate([itself[None], order])
    return jax.vmap(choose)(keys, own).astype(jnp.int32)


def touch_ends(values, stream_key, least, high):
    shape = values.shape
    index_at = [jax.random.randint(jax.random.fold_in(stream_key, axis), (), 0, shape[axis]) for axis in range(len(shape))]
    values = values.at[tuple(index_at)].set(least)
    longest = shape.index(max(shape))
    index_at[longest] = (index_at[longest] + 1) % shape[longest]
    return values.at[tuple(index_at)].set(high)


def shard_levels(rng, extent, cuts, low, largest):
    factor_of, own = 1.0, jax.random.fold_in(rng, 6)
    for position, shards_of in cuts:
        steps = jnp.exp(jax.random.uniform(jax.random.fold_in(own, position), (shards_of,), jnp.float32, low / len(cuts), largest / len(cuts)))
        factor_of = factor_of * jnp.repeat(steps, extent[position] // shards_of).reshape([-1 if axis == position else 1 for axis in range(len(extent))])
    return factor_of


def scatter_about(key, extent, deviation, bound, cuts=(), kind=jnp.bfloat16):
    gain = shard_levels(key, extent, cuts, -0.22, 0.18) if cuts else 1.0
    drawn = jax.random.normal(key, extent, jnp.float32) * deviation * gain
    return jnp.minimum(jnp.maximum(drawn, -bound), bound).astype(kind)


def setup_inputs(seed: int = 0) -> dict:
    splits = jax.random.split(jax.random.key(seed), 9)
    positions = scatter_about(splits[0], (3, CELLS), 1.0, 6.0, ((1, 128),), jnp.float32)
    radius = jnp.clip(jnp.exp(math.log(1.4) - 0.6931472 * jax.random.uniform(splits[1], (CELLS,), jnp.float32) ** shard_levels(splits[1], (CELLS,), ((0, 128),), -0.2, 0.2)), 0.7, 1.4)
    uptake_rate = jnp.clip(jnp.exp(math.log(3.0) - 2.3025851 * jax.random.uniform(splits[2], (CELLS,), jnp.float32) ** shard_levels(splits[2], (CELLS,), ((0, 128),), -0.2, 0.2)), 0.3, 3.0)
    voxel_local = touch_ends(jax.random.randint(splits[3], (CELLS,), 0, CZ * CY * NX), jax.random.fold_in(splits[3], 1), 0, (CZ * CY * NX) - 1).astype(jnp.int32)
    cell_counts = draw_cell_counts(jax.random.fold_in(splits[8], 71), 0)
    send_counts = draw_send_counts(jax.random.fold_in(splits[8], 71), 0)
    neighbor_blocks = draw_neighbor_blocks(jax.random.fold_in(splits[8], 71), 0)
    field = jnp.clip(0.2 + 1.8 * jax.random.uniform(splits[7], (2, NZ, NY, NX), jnp.float32) ** shard_levels(splits[7], (2, NZ, NY, NX), ((1, 8), (2, 16)), -0.2, 0.2), 0.2, 2.0)
    return dict(positions=positions, radius=radius, uptake_rate=uptake_rate, voxel_local=voxel_local, cell_counts=cell_counts, send_counts=send_counts, neighbor_blocks=neighbor_blocks, field=field)


MICHAELIS_HALF = 0.5
HYPOXIA_HALF = 0.6
SECRETION = 0.4
STEP_TIME = 0.5
DIFFUSION = (0.16, 0.12)
DECAY = (0.0, 0.03)
REPULSION = 1.0
ADHESION = 0.35
REPEL_RANGE = 1.0
ADHERE_RANGE = 4.0
FORCE_SCALE = 0.08
CHEMOTAXIS = 1.5


def block_force(mine, others):
    offset = mine[:3, :, :, None, None] - others[:3, :, None, :, :]
    distance = jnp.sum(offset * offset, axis=0)
    strength = REPULSION * jnp.exp(-distance / REPEL_RANGE) - ADHESION * jnp.exp(-distance / ADHERE_RANGE)
    weight = mine[3][:, :, None, None] * others[3][:, None, :, :] * strength
    return jnp.sum(offset * weight[None], axis=(3, 4))


def relax(padded):
    center = padded[:, 1:-1, 1:-1]
    sideways = jnp.pad(center, ((0, 0), (0, 0), (0, 0), (1, 1)))
    beside_all = padded[:, 2:, 1:-1] + padded[:, :-2, 1:-1]
    beside_all = beside_all + padded[:, 1:-1, 2:] + padded[:, 1:-1, :-2]
    beside_all = beside_all + sideways[..., 2:] + sideways[..., :-2]
    spread = jnp.array(DIFFUSION, jnp.float32)[:, None, None, None]
    losses = jnp.array(DECAY, jnp.float32)[:, None, None, None]
    return center + spread * (beside_all - 6.0 * center) - losses * center


def routing(sends, length):
    ends = jnp.cumsum(sends).astype(jnp.int32)
    starts = (ends - sends).astype(jnp.int32)
    cell = jnp.arange(length, dtype=jnp.int32)
    target = jnp.sum((ends[:, None] <= cell[None, :]).astype(jnp.int32), axis=0).astype(jnp.int32)
    routed = target < sends.shape[0]
    target = jnp.minimum(target, sends.shape[0] - 1).astype(jnp.int32)
    lanes = jnp.arange(sends.shape[0], dtype=jnp.int32)
    first = jnp.sum(jnp.where(lanes[:, None] == target[None, :], starts[:, None], 0), axis=0).astype(jnp.int32)
    return target, (cell - first).astype(jnp.int32), routed


def reference(positions, radius, uptake_rate, voxel_local, cell_counts, send_counts, neighbor_blocks, field):
    devices = N_SLAB * N_TILE
    width = HB * 128
    cell = jnp.arange(CAP, dtype=jnp.int32)
    live = cell[None, :] < cell_counts[:, None]
    kept = jnp.where(live, radius.reshape(devices, CAP), 0.0)
    table = jnp.concatenate([positions.reshape(3, devices, CAP), kept[None]], axis=0)
    grid = table.reshape(4, N_SLAB, N_TILE, CAP)
    blank = jnp.zeros((4, N_SLAB, 1, width), jnp.float32)
    lower = jnp.concatenate([blank, grid[:, :, :-1, CAP - width:]], axis=2)
    upper = jnp.concatenate([grid[:, :, 1:, :width], blank], axis=2)
    extended = jnp.concatenate([lower, grid, upper], axis=3).reshape(4, devices, NB + 2 * HB, 128)
    extended = jnp.moveaxis(extended, 1, 0)
    lists = neighbor_blocks.reshape(devices, NB, K)

    def device_force(pair):
        frame, chosen = pair
        mine = frame[:, HB:HB + NB]
        others = jnp.take(frame, chosen.reshape(-1), axis=1).reshape(4, NB, K, 128)
        return block_force(mine, others)

    forces = lax.map(device_force, (extended, lists))
    forces = jnp.moveaxis(forces, 1, 0).reshape(3, devices * CAP)

    target, rank, routed = jax.vmap(lambda sends: routing(sends, CAP))(send_counts)
    slab_of = jnp.broadcast_to((jnp.arange(devices, dtype=jnp.int32) // N_TILE)[:, None], (devices, CAP))
    voxels = voxel_local.reshape(devices, CAP)
    volume = CZ * CY * NX
    blocks = field.reshape(2, N_SLAB, CZ, N_TILE, CY, NX).transpose(1, 3, 0, 2, 4, 5).reshape(N_SLAB, N_TILE, 2, volume)
    oxygen = blocks[slab_of, target, 0, voxels]
    rates = jnp.where(routed, uptake_rate.reshape(devices, CAP), 0.0)
    consume = rates * oxygen / (MICHAELIS_HALF + oxygen)
    secrete = SECRETION * rates * HYPOXIA_HALF / (HYPOXIA_HALF + oxygen)
    blocks = blocks.at[slab_of, target, 0, voxels].add(-STEP_TIME * consume)
    blocks = blocks.at[slab_of, target, 1, voxels].add(STEP_TIME * secrete)
    state = blocks.reshape(N_SLAB, N_TILE, 2, CZ, CY, NX).transpose(2, 0, 3, 1, 4, 5).reshape(2, N_SLAB * CZ, N_TILE * CY, NX)
    for step in range(ITERS):
        state = relax(jnp.pad(state, ((0, 0), (1, 1), (1, 1), (0, 0))))

    vegf = jnp.pad(state[1], 1)
    depth_at = slab_of * CZ + voxels // (CY * NX) + 1
    row_at = target * CY + (voxels // NX) % CY + 1
    column_at = voxels % NX + 1
    rise_z = 0.5 * (vegf[depth_at + 1, row_at, column_at] - vegf[depth_at - 1, row_at, column_at])
    rise_y = 0.5 * (vegf[depth_at, row_at + 1, column_at] - vegf[depth_at, row_at - 1, column_at])
    rise_x = 0.5 * (vegf[depth_at, row_at, column_at + 1] - vegf[depth_at, row_at, column_at - 1])
    slope = jnp.where(routed[None], jnp.stack([rise_z, rise_y, rise_x]), 0.0).reshape(3, devices * CAP)
    velocity = FORCE_SCALE * forces + CHEMOTAXIS * slope
    return velocity, state
```

```python
import jax
import jax.numpy as jnp
from jax import lax
from jax.sharding import PartitionSpec as P

HB = 4
K = 8
ITERS = 4


MICHAELIS_HALF = 0.5
HYPOXIA_HALF = 0.6
SECRETION = 0.4
STEP_TIME = 0.5
DIFFUSION = (0.16, 0.12)
DECAY = (0.0, 0.03)
REPULSION = 1.0
ADHESION = 0.35
REPEL_RANGE = 1.0
ADHERE_RANGE = 4.0
FORCE_SCALE = 0.08
CHEMOTAXIS = 1.5
SLOT_BLOCK = 512


def with_halo(block, sides, width):
    for axis, dim in sides:
        count = lax.axis_size(axis)
        forward = [(i, i + 1) for i in range(count - 1)]
        backward = [(target, source) for source, target in forward]
        low = lax.ppermute(
            lax.slice_in_dim(block, block.shape[dim] - width, None, axis=dim), axis, forward
        )
        high = lax.ppermute(lax.slice_in_dim(block, 0, width, axis=dim), axis, backward)
        block = jnp.concatenate([low, block, high], axis=dim)
    return block


def block_force(mine, others):
    offset = mine[:3, :, :, None, None] - others[:3, :, None, :, :]
    distance = jnp.sum(offset * offset, axis=0)
    strength = REPULSION * jnp.exp(-distance / REPEL_RANGE) - ADHESION * jnp.exp(
        -distance / ADHERE_RANGE
    )
    weight = mine[3][:, :, None, None] * others[3][:, None, :, :] * strength
    return jnp.sum(offset * weight[None], axis=(3, 4))


def relax(padded):
    center = padded[:, 1:-1, 1:-1]
    sideways = jnp.pad(center, ((0, 0), (0, 0), (0, 0), (1, 1)))
    beside_all = padded[:, 2:, 1:-1] + padded[:, :-2, 1:-1]
    beside_all = beside_all + padded[:, 1:-1, 2:] + padded[:, 1:-1, :-2]
    beside_all = beside_all + sideways[..., 2:] + sideways[..., :-2]
    spread = jnp.array(DIFFUSION, jnp.float32)[:, None, None, None]
    losses = jnp.array(DECAY, jnp.float32)[:, None, None, None]
    return center + spread * (beside_all - 6.0 * center) - losses * center


def routing(sends, length):
    ends = jnp.cumsum(sends)
    starts = ends - sends
    cell = jnp.arange(length, dtype=jnp.int32)
    target = jnp.sum((ends[:, None] <= cell[None, :]).astype(jnp.int32), axis=0)
    routed = target < sends.shape[0]
    target = jnp.minimum(target, sends.shape[0] - 1)
    lanes = jnp.arange(sends.shape[0], dtype=jnp.int32)
    first = jnp.sum(jnp.where(lanes[:, None] == target[None, :], starts[:, None], 0), axis=0)
    return (target, cell - first, routed)


def hot_tables(piece, planes, columns):
    row_hot = (piece[:, None] // columns == jnp.arange(planes, dtype=jnp.int32)[None, :]).astype(
        jnp.float32
    )
    column_hot = (piece[:, None] % columns == jnp.arange(columns, dtype=jnp.int32)[None, :]).astype(
        jnp.float32
    )
    return (row_hot, column_hot)


def pick_voxels(fields, reached):
    species, planes, columns = fields.shape
    pieces = reached.reshape(-1, SLOT_BLOCK)

    def one_piece(piece):
        row_hot, column_hot = hot_tables(piece, planes, columns)
        picked = jnp.einsum("srx,mx->srm", fields, column_hot, precision=lax.Precision.HIGHEST)
        return jnp.sum(picked * jnp.transpose(row_hot)[None], axis=1)

    found = lax.map(one_piece, pieces)
    return jnp.moveaxis(found, 1, 0).reshape(species, -1)


def spread_voxels(amounts, reached, planes, columns):
    species = amounts.shape[0]
    pieces = reached.reshape(-1, SLOT_BLOCK)
    shares = jnp.moveaxis(amounts.reshape(species, -1, SLOT_BLOCK), 1, 0)

    def add_piece(total, item):
        piece, share = item
        row_hot, column_hot = hot_tables(piece, planes, columns)
        weighted = share[:, :, None] * row_hot[None]
        return (
            total
            + jnp.einsum("smr,mx->srx", weighted, column_hot, precision=lax.Precision.HIGHEST),
            None,
        )

    empty = jnp.zeros((species, planes, columns), jnp.float32)
    total, unused = lax.scan(add_piece, empty, (pieces, shares))
    return total


def neighbours(block, axis, dim):
    count = lax.axis_size(axis)
    forward = [(i, i + 1) for i in range(count - 1)]
    backward = [(target, source) for source, target in forward]
    low = lax.ppermute(lax.slice_in_dim(block, block.shape[dim] - 1, None, axis=dim), axis, forward)
    high = lax.ppermute(lax.slice_in_dim(block, 0, 1, axis=dim), axis, backward)
    return (low, high)


def shifted(block, low, high, dim):
    size = block.shape[dim]
    up = jnp.concatenate([lax.slice_in_dim(block, 1, size, axis=dim), high], axis=dim)
    down = jnp.concatenate([low, lax.slice_in_dim(block, 0, size - 1, axis=dim)], axis=dim)
    return (up, down)


def relax_step(center):
    z_low, z_high = neighbours(center, "slab", 1)
    y_low, y_high = neighbours(center, "tile", 2)
    z_up, z_down = shifted(center, z_low, z_high, 1)
    y_up, y_down = shifted(center, y_low, y_high, 2)
    sideways = jnp.pad(center, ((0, 0), (0, 0), (0, 0), (1, 1)))
    beside_all = z_up + z_down
    beside_all = beside_all + y_up + y_down
    beside_all = beside_all + sideways[..., 2:] + sideways[..., :-2]
    spread = jnp.array(DIFFUSION, jnp.float32)[:, None, None, None]
    losses = jnp.array(DECAY, jnp.float32)[:, None, None, None]
    return center + spread * (beside_all - 6.0 * center) - losses * center


def bits_of(width):
    return max(1, (width - 1).bit_length())


def gather_windows(values, starts, length):
    channels, cells = values.shape
    width = cells + length
    rows = starts.shape[0]
    padded = jnp.pad(values, ((0, 0), (0, length)))
    held = jnp.broadcast_to(padded[:, None, :], (channels, rows, width))
    for bit in range(bits_of(width)):
        step = 1 << bit
        take = ((starts >> bit) & 1 == 1)[None, :, None]
        held = jnp.where(take, jnp.roll(held, -step, axis=2), held)
    return held[:, :, :length]


def scatter_windows(windows, starts, cells):
    channels, rows, length = windows.shape
    width = cells + length
    held = jnp.pad(windows, ((0, 0), (0, 0), (0, width - length)))
    for bit in range(bits_of(width)):
        step = 1 << bit
        take = ((starts >> bit) & 1 == 1)[None, :, None]
        held = jnp.where(take, jnp.roll(held, step, axis=2), held)
    return jnp.sum(held[:, :, :cells], axis=1)


def local(
    positions, radius, uptake_rate, voxel_local, cell_counts, send_counts, neighbor_blocks, field
):
    tiles = lax.axis_size("tile")
    capacity = positions.shape[1]
    blocks = capacity // 128
    slot_size = 2 * capacity // tiles
    cell = jnp.arange(capacity, dtype=jnp.int32)
    count = cell_counts[0]
    kept = jnp.where(cell < count, radius, 0.0)
    table = jnp.concatenate([positions, kept[None]], axis=0)
    extended = with_halo(table, (("tile", 1),), HB * 128)
    extended = extended.reshape(4, blocks + 2 * HB, 128)
    group = 4
    parts = []
    for first in range(0, blocks, group):
        chosen = neighbor_blocks[first:first + group]
        mine = extended[:, first + HB:first + HB + group]
        others = jnp.take(extended, chosen.reshape(-1), axis=1).reshape(4, group, K, 128)
        parts.append(block_force(mine, others))
    forces = jnp.concatenate(parts, axis=1).reshape(3, capacity)
    sends = send_counts[0]
    ends = jnp.cumsum(sends)
    starts = ends - sends
    ranks = jnp.arange(slot_size, dtype=jnp.int32)
    valid = ranks[None, :] < sends[:, None]
    payload = jnp.stack([voxel_local.astype(jnp.float32), uptake_rate])
    windows = gather_windows(payload, starts, slot_size)
    windows = jnp.where(valid[None], windows, 0.0)
    arrived = lax.all_to_all(windows, "tile", split_axis=1, concat_axis=1, tiled=True)
    reached = arrived[0].reshape(-1).astype(jnp.int32)
    rates = arrived[1].reshape(-1)
    species, depth, rows, columns = field.shape
    planes = depth * rows
    oxygen_rows = field[0].reshape(1, planes, columns)
    oxygen = pick_voxels(oxygen_rows, reached)[0]
    consume = rates * oxygen / (MICHAELIS_HALF + oxygen)
    secrete = SECRETION * rates * HYPOXIA_HALF / (HYPOXIA_HALF + oxygen)
    amounts = jnp.stack([-STEP_TIME * consume, STEP_TIME * secrete])
    added = spread_voxels(amounts, reached, planes, columns)
    state = field + added.reshape(species, depth, rows, columns)
    for step in range(ITERS):
        state = relax_step(state)
    vegf = state[1]
    z_low, z_high = neighbours(vegf, "slab", 0)
    y_low, y_high = neighbours(vegf, "tile", 1)
    z_up, z_down = shifted(vegf, z_low, z_high, 0)
    y_up, y_down = shifted(vegf, y_low, y_high, 1)
    rise_z = 0.5 * (z_up - z_down)
    rise_y = 0.5 * (y_up - y_down)
    middle = jnp.pad(vegf, ((0, 0), (0, 0), (1, 1)))
    rise_x = 0.5 * (middle[..., 2:] - middle[..., :-2])
    rises = jnp.stack([rise_z, rise_y, rise_x]).reshape(3, planes, columns)
    slopes = pick_voxels(rises, reached).reshape(3, tiles, slot_size)
    returned = lax.all_to_all(slopes, "tile", split_axis=1, concat_axis=1, tiled=True)
    returned = jnp.where(valid[None], returned, 0.0)
    slope = scatter_windows(returned, starts, capacity)
    velocity = FORCE_SCALE * forces + CHEMOTAXIS * slope
    return (velocity, state)


def solution(mesh):
    placed = (
        P(None, ("slab", "tile")),
        P(("slab", "tile")),
        P(("slab", "tile")),
        P(("slab", "tile")),
        P(("slab", "tile")),
        P(("slab", "tile"), None),
        P(("slab", "tile"), None),
        P(None, "slab", "tile", None),
    )
    return jax.shard_map(
        local,
        mesh=mesh,
        in_specs=placed,
        out_specs=(P(None, ("slab", "tile")), P(None, "slab", "tile", None)),
        check_vma=False,
    )
```

```python
import jax
import jax.numpy as jnp
from jax import lax
from jax.experimental import pallas as pl
from jax.experimental.pallas import tpu as pltpu
from jax.sharding import PartitionSpec as P

HB = 4
K = 8
ITERS = 4


MICHAELIS_HALF = 0.5
HYPOXIA_HALF = 0.6
SECRETION = 0.4
STEP_TIME = 0.5
DIFFUSION = (0.16, 0.12)
DECAY = (0.0, 0.03)
REPULSION = 1.0
ADHESION = 0.35
REPEL_RANGE = 1.0
ADHERE_RANGE = 4.0
FORCE_SCALE = 0.08
CHEMOTAXIS = 1.5
SLOT_BLOCK = 512


def with_halo(block, sides, width):
    for axis, dim in sides:
        count = lax.axis_size(axis)
        forward = [(i, i + 1) for i in range(count - 1)]
        backward = [(target, source) for source, target in forward]
        low = lax.ppermute(
            lax.slice_in_dim(block, block.shape[dim] - width, None, axis=dim), axis, forward
        )
        high = lax.ppermute(lax.slice_in_dim(block, 0, width, axis=dim), axis, backward)
        block = jnp.concatenate([low, block, high], axis=dim)
    return block


def block_force(mine, others):
    offset = mine[:3, :, :, None, None] - others[:3, :, None, :, :]
    distance = jnp.sum(offset * offset, axis=0)
    strength = REPULSION * jnp.exp(-distance / REPEL_RANGE) - ADHESION * jnp.exp(
        -distance / ADHERE_RANGE
    )
    weight = mine[3][:, :, None, None] * others[3][:, None, :, :] * strength
    return jnp.sum(offset * weight[None], axis=(3, 4))


def relax(padded):
    center = padded[:, 1:-1, 1:-1]
    sideways = jnp.pad(center, ((0, 0), (0, 0), (0, 0), (1, 1)))
    beside_all = padded[:, 2:, 1:-1] + padded[:, :-2, 1:-1]
    beside_all = beside_all + padded[:, 1:-1, 2:] + padded[:, 1:-1, :-2]
    beside_all = beside_all + sideways[..., 2:] + sideways[..., :-2]
    spread = jnp.array(DIFFUSION, jnp.float32)[:, None, None, None]
    losses = jnp.array(DECAY, jnp.float32)[:, None, None, None]
    return center + spread * (beside_all - 6.0 * center) - losses * center


def routing(sends, length):
    ends = jnp.cumsum(sends)
    starts = ends - sends
    cell = jnp.arange(length, dtype=jnp.int32)
    target = jnp.sum((ends[:, None] <= cell[None, :]).astype(jnp.int32), axis=0)
    routed = target < sends.shape[0]
    target = jnp.minimum(target, sends.shape[0] - 1)
    lanes = jnp.arange(sends.shape[0], dtype=jnp.int32)
    first = jnp.sum(jnp.where(lanes[:, None] == target[None, :], starts[:, None], 0), axis=0)
    return (target, cell - first, routed)


def hot_tables(piece, planes, columns):
    row_hot = (piece[:, None] // columns == jnp.arange(planes, dtype=jnp.int32)[None, :]).astype(
        jnp.float32
    )
    column_hot = (piece[:, None] % columns == jnp.arange(columns, dtype=jnp.int32)[None, :]).astype(
        jnp.float32
    )
    return (row_hot, column_hot)


def pick_voxels(fields, reached):
    species, planes, columns = fields.shape
    pieces = reached.reshape(-1, SLOT_BLOCK)

    def one_piece(piece):
        row_hot, column_hot = hot_tables(piece, planes, columns)
        picked = jnp.einsum("srx,mx->srm", fields, column_hot, precision=lax.Precision.HIGHEST)
        return jnp.sum(picked * jnp.transpose(row_hot)[None], axis=1)

    found = lax.map(one_piece, pieces)
    return jnp.moveaxis(found, 1, 0).reshape(species, -1)


def spread_voxels(amounts, reached, planes, columns):
    species = amounts.shape[0]
    pieces = reached.reshape(-1, SLOT_BLOCK)
    shares = jnp.moveaxis(amounts.reshape(species, -1, SLOT_BLOCK), 1, 0)

    def add_piece(total, item):
        piece, share = item
        row_hot, column_hot = hot_tables(piece, planes, columns)
        weighted = share[:, :, None] * row_hot[None]
        return (
            total
            + jnp.einsum("smr,mx->srx", weighted, column_hot, precision=lax.Precision.HIGHEST),
            None,
        )

    empty = jnp.zeros((species, planes, columns), jnp.float32)
    total, unused = lax.scan(add_piece, empty, (pieces, shares))
    return total


def force_kernel(chosen_ref, rows_ref, cols_ref, out_ref):
    blocks = out_ref.shape[0]
    picks = chosen_ref.shape[0] // blocks
    chunks = cols_ref.shape[2] // 8
    shape = (8, cols_ref.shape[3])

    def one_block(block, carry):
        own = rows_ref[block + HB]
        mine = [jnp.broadcast_to(own[axis:axis + 1, :], shape) for axis in range(4)]

        def one_pick(pick, totals):
            other = chosen_ref[block * picks + pick]
            totals = list(totals)
            for chunk in range(chunks):
                part = pl.ds(chunk * 8, 8)
                offset = [mine[axis] - cols_ref[other, axis, part, :] for axis in range(3)]
                distance = offset[0] * offset[0] + offset[1] * offset[1] + offset[2] * offset[2]
                strength = REPULSION * jnp.exp(-distance / REPEL_RANGE) - ADHESION * jnp.exp(
                    -distance / ADHERE_RANGE
                )
                weight = mine[3] * cols_ref[other, 3, part, :] * strength
                for axis in range(3):
                    totals[axis] = totals[axis] + offset[axis] * weight
            return tuple(totals)

        zero = jnp.zeros(shape, jnp.float32)
        totals = lax.fori_loop(0, picks, one_pick, (zero, zero, zero))
        out_ref[block] = jnp.concatenate(
            [jnp.sum(total, axis=0, keepdims=True) for total in totals], axis=0
        )
        return carry

    lax.fori_loop(0, blocks, one_block, 0)


def pair_forces(extended, neighbor_blocks):
    coords, span, lanes = extended.shape
    blocks, picks = neighbor_blocks.shape
    rows = jnp.transpose(extended, (1, 0, 2))
    cols = jnp.broadcast_to(rows[:, :, :, None], (span, coords, lanes, lanes))
    pairs = blocks * picks * lanes * lanes
    out = pl.pallas_call(
        force_kernel,
        out_shape=jax.ShapeDtypeStruct((blocks, 3, lanes), jnp.float32),
        in_specs=[
            pl.BlockSpec(memory_space=pltpu.SMEM),
            pl.BlockSpec(memory_space=pltpu.VMEM),
            pl.BlockSpec(memory_space=pltpu.VMEM),
        ],
        out_specs=pl.BlockSpec(memory_space=pltpu.VMEM),
        cost_estimate=pl.CostEstimate(
            flops=26 * pairs, transcendentals=2 * pairs, bytes_accessed=4 * cols.size
        ),
    )(neighbor_blocks.reshape(-1), rows, cols)
    return jnp.transpose(out, (1, 0, 2))


def neighbours(block, axis, dim):
    count = lax.axis_size(axis)
    forward = [(i, i + 1) for i in range(count - 1)]
    backward = [(target, source) for source, target in forward]
    low = lax.ppermute(lax.slice_in_dim(block, block.shape[dim] - 1, None, axis=dim), axis, forward)
    high = lax.ppermute(lax.slice_in_dim(block, 0, 1, axis=dim), axis, backward)
    return (low, high)


def shifted(block, low, high, dim):
    size = block.shape[dim]
    up = jnp.concatenate([lax.slice_in_dim(block, 1, size, axis=dim), high], axis=dim)
    down = jnp.concatenate([low, lax.slice_in_dim(block, 0, size - 1, axis=dim)], axis=dim)
    return (up, down)


def relax_step(center):
    z_low, z_high = neighbours(center, "slab", 1)
    y_low, y_high = neighbours(center, "tile", 2)
    z_up, z_down = shifted(center, z_low, z_high, 1)
    y_up, y_down = shifted(center, y_low, y_high, 2)
    sideways = jnp.pad(center, ((0, 0), (0, 0), (0, 0), (1, 1)))
    beside_all = z_up + z_down
    beside_all = beside_all + y_up + y_down
    beside_all = beside_all + sideways[..., 2:] + sideways[..., :-2]
    spread = jnp.array(DIFFUSION, jnp.float32)[:, None, None, None]
    losses = jnp.array(DECAY, jnp.float32)[:, None, None, None]
    return center + spread * (beside_all - 6.0 * center) - losses * center


def bits_of(width):
    return max(1, (width - 1).bit_length())


def gather_windows(values, starts, length):
    channels, cells = values.shape
    width = cells + length
    rows = starts.shape[0]
    padded = jnp.pad(values, ((0, 0), (0, length)))
    held = jnp.broadcast_to(padded[:, None, :], (channels, rows, width))
    for bit in range(bits_of(width)):
        step = 1 << bit
        take = ((starts >> bit) & 1 == 1)[None, :, None]
        held = jnp.where(take, jnp.roll(held, -step, axis=2), held)
    return held[:, :, :length]


def scatter_windows(windows, starts, cells):
    channels, rows, length = windows.shape
    width = cells + length
    held = jnp.pad(windows, ((0, 0), (0, 0), (0, width - length)))
    for bit in range(bits_of(width)):
        step = 1 << bit
        take = ((starts >> bit) & 1 == 1)[None, :, None]
        held = jnp.where(take, jnp.roll(held, step, axis=2), held)
    return jnp.sum(held[:, :, :cells], axis=1)


def local(
    positions, radius, uptake_rate, voxel_local, cell_counts, send_counts, neighbor_blocks, field
):
    tiles = lax.axis_size("tile")
    capacity = positions.shape[1]
    blocks = capacity // 128
    slot_size = 2 * capacity // tiles
    cell = jnp.arange(capacity, dtype=jnp.int32)
    count = cell_counts[0]
    kept = jnp.where(cell < count, radius, 0.0)
    table = jnp.concatenate([positions, kept[None]], axis=0)
    extended = with_halo(table, (("tile", 1),), HB * 128)
    extended = extended.reshape(4, blocks + 2 * HB, 128)
    forces = pair_forces(extended, neighbor_blocks).reshape(3, capacity)
    sends = send_counts[0]
    ends = jnp.cumsum(sends)
    starts = ends - sends
    ranks = jnp.arange(slot_size, dtype=jnp.int32)
    valid = ranks[None, :] < sends[:, None]
    payload = jnp.stack([voxel_local.astype(jnp.float32), uptake_rate])
    windows = gather_windows(payload, starts, slot_size)
    windows = jnp.where(valid[None], windows, 0.0)
    arrived = lax.all_to_all(windows, "tile", split_axis=1, concat_axis=1, tiled=True)
    reached = arrived[0].reshape(-1).astype(jnp.int32)
    rates = arrived[1].reshape(-1)
    species, depth, rows, columns = field.shape
    planes = depth * rows
    oxygen_rows = field[0].reshape(1, planes, columns)
    oxygen = pick_voxels(oxygen_rows, reached)[0]
    consume = rates * oxygen / (MICHAELIS_HALF + oxygen)
    secrete = SECRETION * rates * HYPOXIA_HALF / (HYPOXIA_HALF + oxygen)
    amounts = jnp.stack([-STEP_TIME * consume, STEP_TIME * secrete])
    added = spread_voxels(amounts, reached, planes, columns)
    state = field + added.reshape(species, depth, rows, columns)
    for step in range(ITERS):
        state = relax_step(state)
    vegf = state[1]
    z_low, z_high = neighbours(vegf, "slab", 0)
    y_low, y_high = neighbours(vegf, "tile", 1)
    z_up, z_down = shifted(vegf, z_low, z_high, 0)
    y_up, y_down = shifted(vegf, y_low, y_high, 1)
    rise_z = 0.5 * (z_up - z_down)
    rise_y = 0.5 * (y_up - y_down)
    middle = jnp.pad(vegf, ((0, 0), (0, 0), (1, 1)))
    rise_x = 0.5 * (middle[..., 2:] - middle[..., :-2])
    rises = jnp.stack([rise_z, rise_y, rise_x]).reshape(3, planes, columns)
    slopes = pick_voxels(rises, reached).reshape(3, tiles, slot_size)
    returned = lax.all_to_all(slopes, "tile", split_axis=1, concat_axis=1, tiled=True)
    returned = jnp.where(valid[None], returned, 0.0)
    slope = scatter_windows(returned, starts, capacity)
    velocity = FORCE_SCALE * forces + CHEMOTAXIS * slope
    return (velocity, state)


def solution(mesh):
    placed = (
        P(None, ("slab", "tile")),
        P(("slab", "tile")),
        P(("slab", "tile")),
        P(("slab", "tile")),
        P(("slab", "tile")),
        P(("slab", "tile"), None),
        P(("slab", "tile"), None),
        P(None, "slab", "tile", None),
    )
    return jax.shard_map(
        local,
        mesh=mesh,
        in_specs=placed,
        out_specs=(P(None, ("slab", "tile")), P(None, "slab", "tile", None)),
        check_vma=False,
    )
```

```python
import jax
import jax.numpy as jnp
from jax import lax
from jax.experimental import pallas as pl
from jax.experimental.pallas import tpu as pltpu
from jax.sharding import PartitionSpec as P

HB = 4
K = 8
ITERS = 4


MICHAELIS_HALF = 0.5
HYPOXIA_HALF = 0.6
SECRETION = 0.4
STEP_TIME = 0.5
DIFFUSION = (0.16, 0.12)
DECAY = (0.0, 0.03)
REPULSION = 1.0
ADHESION = 0.35
REPEL_RANGE = 1.0
ADHERE_RANGE = 4.0
FORCE_SCALE = 0.08
CHEMOTAXIS = 1.5
SLOT_BLOCK = 1024


def with_halo(block, sides, width):
    for axis, dim in sides:
        count = lax.axis_size(axis)
        forward = [(i, i + 1) for i in range(count - 1)]
        backward = [(target, source) for source, target in forward]
        low = lax.ppermute(
            lax.slice_in_dim(block, block.shape[dim] - width, None, axis=dim), axis, forward
        )
        high = lax.ppermute(lax.slice_in_dim(block, 0, width, axis=dim), axis, backward)
        block = jnp.concatenate([low, block, high], axis=dim)
    return block


def block_force(mine, others):
    offset = mine[:3, :, :, None, None] - others[:3, :, None, :, :]
    distance = jnp.sum(offset * offset, axis=0)
    strength = REPULSION * jnp.exp(-distance / REPEL_RANGE) - ADHESION * jnp.exp(
        -distance / ADHERE_RANGE
    )
    weight = mine[3][:, :, None, None] * others[3][:, None, :, :] * strength
    return jnp.sum(offset * weight[None], axis=(3, 4))


def relax(padded):
    center = padded[:, 1:-1, 1:-1]
    sideways = jnp.pad(center, ((0, 0), (0, 0), (0, 0), (1, 1)))
    beside_all = padded[:, 2:, 1:-1] + padded[:, :-2, 1:-1]
    beside_all = beside_all + padded[:, 1:-1, 2:] + padded[:, 1:-1, :-2]
    beside_all = beside_all + sideways[..., 2:] + sideways[..., :-2]
    spread = jnp.array(DIFFUSION, jnp.float32)[:, None, None, None]
    losses = jnp.array(DECAY, jnp.float32)[:, None, None, None]
    return center + spread * (beside_all - 6.0 * center) - losses * center


def routing(sends, length):
    ends = jnp.cumsum(sends)
    starts = ends - sends
    cell = jnp.arange(length, dtype=jnp.int32)
    target = jnp.sum((ends[:, None] <= cell[None, :]).astype(jnp.int32), axis=0)
    routed = target < sends.shape[0]
    target = jnp.minimum(target, sends.shape[0] - 1)
    lanes = jnp.arange(sends.shape[0], dtype=jnp.int32)
    first = jnp.sum(jnp.where(lanes[:, None] == target[None, :], starts[:, None], 0), axis=0)
    return (target, cell - first, routed)


def hot_tables(piece, planes, columns, kind=jnp.float32):
    row_hot = (piece[:, None] // columns == jnp.arange(planes, dtype=jnp.int32)[None, :]).astype(
        kind
    )
    column_hot = (piece[:, None] % columns == jnp.arange(columns, dtype=jnp.int32)[None, :]).astype(
        kind
    )
    return (row_hot, column_hot)


def split_three(values):
    high = lax.reduce_precision(values, exponent_bits=8, mantissa_bits=7)
    rest = values - high
    middle = lax.reduce_precision(rest, exponent_bits=8, mantissa_bits=7)
    return jnp.stack([high, middle, rest - middle]).astype(jnp.bfloat16)


def pick_voxels(fields, reached):
    species, planes, columns = fields.shape
    parts = split_three(fields)
    pieces = reached.reshape(-1, SLOT_BLOCK)

    def one_piece(piece):
        row_hot, column_hot = hot_tables(piece, planes, columns, jnp.bfloat16)
        picked = jnp.einsum(
            "psrx,mx->psrm", parts, column_hot, preferred_element_type=jnp.float32
        )
        picked = picked[0] + picked[1] + picked[2]
        return jnp.sum(picked * jnp.transpose(row_hot).astype(jnp.float32)[None], axis=1)

    found = lax.map(one_piece, pieces)
    return jnp.moveaxis(found, 1, 0).reshape(species, -1)


def spread_voxels(amounts, reached, planes, columns):
    species = amounts.shape[0]
    pieces = reached.reshape(-1, SLOT_BLOCK)
    shares = jnp.moveaxis(amounts.reshape(species, -1, SLOT_BLOCK), 1, 0)

    def add_piece(total, item):
        piece, share = item
        row_hot, column_hot = hot_tables(piece, planes, columns)
        weighted = share[:, :, None] * row_hot[None]
        return (
            total
            + jnp.einsum("smr,mx->srx", weighted, column_hot, precision=lax.Precision.HIGHEST),
            None,
        )

    empty = jnp.zeros((species, planes, columns), jnp.float32)
    total, unused = lax.scan(add_piece, empty, (pieces, shares))
    return total


def force_kernel(chosen_ref, rows_ref, cols_ref, out_ref):
    blocks = out_ref.shape[0]
    picks = chosen_ref.shape[0] // blocks
    chunks = cols_ref.shape[2] // 8
    shape = (8, cols_ref.shape[3])

    def one_block(block, carry):
        own = rows_ref[block + HB]
        mine = [jnp.broadcast_to(own[axis:axis + 1, :], shape) for axis in range(4)]

        def one_pick(pick, totals):
            other = chosen_ref[block * picks + pick]
            totals = list(totals)
            for chunk in range(chunks):
                part = pl.ds(chunk * 8, 8)
                offset = [mine[axis] - cols_ref[other, axis, part, :] for axis in range(3)]
                distance = offset[0] * offset[0] + offset[1] * offset[1] + offset[2] * offset[2]
                strength = REPULSION * jnp.exp(-distance / REPEL_RANGE) - ADHESION * jnp.exp(
                    -distance / ADHERE_RANGE
                )
                weight = mine[3] * cols_ref[other, 3, part, :] * strength
                for axis in range(3):
                    totals[axis] = totals[axis] + offset[axis] * weight
            return tuple(totals)

        zero = jnp.zeros(shape, jnp.float32)
        totals = lax.fori_loop(0, picks, one_pick, (zero, zero, zero))
        out_ref[block] = jnp.concatenate(
            [jnp.sum(total, axis=0, keepdims=True) for total in totals], axis=0
        )
        return carry

    lax.fori_loop(0, blocks, one_block, 0)


def pair_forces(extended, neighbor_blocks):
    coords, span, lanes = extended.shape
    blocks, picks = neighbor_blocks.shape
    rows = jnp.transpose(extended, (1, 0, 2))
    cols = jnp.broadcast_to(rows[:, :, :, None], (span, coords, lanes, lanes))
    pairs = blocks * picks * lanes * lanes
    out = pl.pallas_call(
        force_kernel,
        out_shape=jax.ShapeDtypeStruct((blocks, 3, lanes), jnp.float32),
        in_specs=[
            pl.BlockSpec(memory_space=pltpu.SMEM),
            pl.BlockSpec(memory_space=pltpu.VMEM),
            pl.BlockSpec(memory_space=pltpu.VMEM),
        ],
        out_specs=pl.BlockSpec(memory_space=pltpu.VMEM),
        cost_estimate=pl.CostEstimate(
            flops=26 * pairs, transcendentals=2 * pairs, bytes_accessed=4 * cols.size
        ),
    )(neighbor_blocks.reshape(-1), rows, cols)
    return jnp.transpose(out, (1, 0, 2))


def neighbours(block, axis, dim):
    count = lax.axis_size(axis)
    forward = [(i, i + 1) for i in range(count - 1)]
    backward = [(target, source) for source, target in forward]
    low = lax.ppermute(lax.slice_in_dim(block, block.shape[dim] - 1, None, axis=dim), axis, forward)
    high = lax.ppermute(lax.slice_in_dim(block, 0, 1, axis=dim), axis, backward)
    return (low, high)


def shifted(block, low, high, dim):
    size = block.shape[dim]
    up = jnp.concatenate([lax.slice_in_dim(block, 1, size, axis=dim), high], axis=dim)
    down = jnp.concatenate([low, lax.slice_in_dim(block, 0, size - 1, axis=dim)], axis=dim)
    return (up, down)


def relax_step(center):
    z_low, z_high = neighbours(center, "slab", 1)
    y_low, y_high = neighbours(center, "tile", 2)
    z_up, z_down = shifted(center, z_low, z_high, 1)
    y_up, y_down = shifted(center, y_low, y_high, 2)
    sideways = jnp.pad(center, ((0, 0), (0, 0), (0, 0), (1, 1)))
    beside_all = z_up + z_down
    beside_all = beside_all + y_up + y_down
    beside_all = beside_all + sideways[..., 2:] + sideways[..., :-2]
    spread = jnp.array(DIFFUSION, jnp.float32)[:, None, None, None]
    losses = jnp.array(DECAY, jnp.float32)[:, None, None, None]
    return center + spread * (beside_all - 6.0 * center) - losses * center


def bits_of(width):
    return max(1, (width - 1).bit_length())


def gather_windows(values, starts, length):
    channels, cells = values.shape
    width = cells + length
    rows = starts.shape[0]
    padded = jnp.pad(values, ((0, 0), (0, length)))
    held = jnp.broadcast_to(padded[:, None, :], (channels, rows, width))
    for bit in range(bits_of(width)):
        step = 1 << bit
        take = ((starts >> bit) & 1 == 1)[None, :, None]
        held = jnp.where(take, jnp.roll(held, -step, axis=2), held)
    return held[:, :, :length]


def scatter_windows(windows, starts, cells):
    channels, rows, length = windows.shape
    width = cells + length
    held = jnp.pad(windows, ((0, 0), (0, 0), (0, width - length)))
    for bit in range(bits_of(width)):
        step = 1 << bit
        take = ((starts >> bit) & 1 == 1)[None, :, None]
        held = jnp.where(take, jnp.roll(held, step, axis=2), held)
    return jnp.sum(held[:, :, :cells], axis=1)


def local(
    positions, radius, uptake_rate, voxel_local, cell_counts, send_counts, neighbor_blocks, field
):
    tiles = lax.axis_size("tile")
    capacity = positions.shape[1]
    blocks = capacity // 128
    slot_size = 2 * capacity // tiles
    cell = jnp.arange(capacity, dtype=jnp.int32)
    count = cell_counts[0]
    kept = jnp.where(cell < count, radius, 0.0)
    table = jnp.concatenate([positions, kept[None]], axis=0)
    extended = with_halo(table, (("tile", 1),), HB * 128)
    extended = extended.reshape(4, blocks + 2 * HB, 128)
    forces = pair_forces(extended, neighbor_blocks).reshape(3, capacity)
    sends = send_counts[0]
    ends = jnp.cumsum(sends)
    starts = ends - sends
    ranks = jnp.arange(slot_size, dtype=jnp.int32)
    valid = ranks[None, :] < sends[:, None]
    payload = jnp.stack([voxel_local.astype(jnp.float32), uptake_rate])
    windows = gather_windows(payload, starts, slot_size)
    windows = jnp.where(valid[None], windows, 0.0)
    arrived = lax.all_to_all(windows, "tile", split_axis=1, concat_axis=1, tiled=True)
    reached = arrived[0].reshape(-1).astype(jnp.int32)
    rates = arrived[1].reshape(-1)
    species, depth, rows, columns = field.shape
    planes = depth * rows
    oxygen_rows = field[0].reshape(1, planes, columns)
    oxygen = pick_voxels(oxygen_rows, reached)[0]
    consume = rates * oxygen / (MICHAELIS_HALF + oxygen)
    secrete = SECRETION * rates * HYPOXIA_HALF / (HYPOXIA_HALF + oxygen)
    amounts = jnp.stack([-STEP_TIME * consume, STEP_TIME * secrete])
    added = spread_voxels(amounts, reached, planes, columns)
    state = field + added.reshape(species, depth, rows, columns)
    for step in range(ITERS):
        state = relax_step(state)
    vegf = state[1]
    z_low, z_high = neighbours(vegf, "slab", 0)
    y_low, y_high = neighbours(vegf, "tile", 1)
    z_up, z_down = shifted(vegf, z_low, z_high, 0)
    y_up, y_down = shifted(vegf, y_low, y_high, 1)
    rise_z = 0.5 * (z_up - z_down)
    rise_y = 0.5 * (y_up - y_down)
    middle = jnp.pad(vegf, ((0, 0), (0, 0), (1, 1)))
    rise_x = 0.5 * (middle[..., 2:] - middle[..., :-2])
    rises = jnp.stack([rise_z, rise_y, rise_x]).reshape(3, planes, columns)
    slopes = pick_voxels(rises, reached).reshape(3, tiles, slot_size)
    returned = lax.all_to_all(slopes, "tile", split_axis=1, concat_axis=1, tiled=True)
    returned = jnp.where(valid[None], returned, 0.0)
    slope = scatter_windows(returned, starts, capacity)
    velocity = FORCE_SCALE * forces + CHEMOTAXIS * slope
    return (velocity, state)


def solution(mesh):
    placed = (
        P(None, ("slab", "tile")),
        P(("slab", "tile")),
        P(("slab", "tile")),
        P(("slab", "tile")),
        P(("slab", "tile")),
        P(("slab", "tile"), None),
        P(("slab", "tile"), None),
        P(None, "slab", "tile", None),
    )
    return jax.shard_map(
        local,
        mesh=mesh,
        in_specs=placed,
        out_specs=(P(None, ("slab", "tile")), P(None, "slab", "tile", None)),
        check_vma=False,
    )
```

```python
import jax
import jax.numpy as jnp
from jax import lax
from jax.experimental import pallas as pl
from jax.experimental.pallas import tpu as pltpu
from jax.sharding import PartitionSpec as P

HB = 4
K = 8
ITERS = 4


MICHAELIS_HALF = 0.5
HYPOXIA_HALF = 0.6
SECRETION = 0.4
STEP_TIME = 0.5
DIFFUSION = (0.16, 0.12)
DECAY = (0.0, 0.03)
REPULSION = 1.0
ADHESION = 0.35
REPEL_RANGE = 1.0
ADHERE_RANGE = 4.0
FORCE_SCALE = 0.08
CHEMOTAXIS = 1.5
SLOT_BLOCK = 512


def with_halo(block, sides, width):
    for axis, dim in sides:
        count = lax.axis_size(axis)
        forward = [(i, i + 1) for i in range(count - 1)]
        backward = [(target, source) for source, target in forward]
        low = lax.ppermute(
            lax.slice_in_dim(block, block.shape[dim] - width, None, axis=dim), axis, forward
        )
        high = lax.ppermute(lax.slice_in_dim(block, 0, width, axis=dim), axis, backward)
        block = jnp.concatenate([low, block, high], axis=dim)
    return block


def block_force(mine, others):
    offset = mine[:3, :, :, None, None] - others[:3, :, None, :, :]
    distance = jnp.sum(offset * offset, axis=0)
    strength = REPULSION * jnp.exp(-distance / REPEL_RANGE) - ADHESION * jnp.exp(
        -distance / ADHERE_RANGE
    )
    weight = mine[3][:, :, None, None] * others[3][:, None, :, :] * strength
    return jnp.sum(offset * weight[None], axis=(3, 4))


def relax(padded):
    center = padded[:, 1:-1, 1:-1]
    sideways = jnp.pad(center, ((0, 0), (0, 0), (0, 0), (1, 1)))
    beside_all = padded[:, 2:, 1:-1] + padded[:, :-2, 1:-1]
    beside_all = beside_all + padded[:, 1:-1, 2:] + padded[:, 1:-1, :-2]
    beside_all = beside_all + sideways[..., 2:] + sideways[..., :-2]
    spread = jnp.array(DIFFUSION, jnp.float32)[:, None, None, None]
    losses = jnp.array(DECAY, jnp.float32)[:, None, None, None]
    return center + spread * (beside_all - 6.0 * center) - losses * center


def routing(sends, length):
    ends = jnp.cumsum(sends)
    starts = ends - sends
    cell = jnp.arange(length, dtype=jnp.int32)
    target = jnp.sum((ends[:, None] <= cell[None, :]).astype(jnp.int32), axis=0)
    routed = target < sends.shape[0]
    target = jnp.minimum(target, sends.shape[0] - 1)
    lanes = jnp.arange(sends.shape[0], dtype=jnp.int32)
    first = jnp.sum(jnp.where(lanes[:, None] == target[None, :], starts[:, None], 0), axis=0)
    return (target, cell - first, routed)


def hot_tables(piece, planes, columns, kind=jnp.float32):
    row_hot = (piece[:, None] // columns == jnp.arange(planes, dtype=jnp.int32)[None, :]).astype(
        kind
    )
    column_hot = (piece[:, None] % columns == jnp.arange(columns, dtype=jnp.int32)[None, :]).astype(
        kind
    )
    return (row_hot, column_hot)


def split_three(values):
    high = lax.reduce_precision(values, exponent_bits=8, mantissa_bits=7)
    rest = values - high
    middle = lax.reduce_precision(rest, exponent_bits=8, mantissa_bits=7)
    return jnp.stack([high, middle, rest - middle]).astype(jnp.bfloat16)


def pick_exact(fields, reached, block):
    species, planes, columns = fields.shape
    parts = split_three(fields)
    pieces = reached.reshape(-1, block)

    def one_piece(piece):
        row_hot, column_hot = hot_tables(piece, planes, columns, jnp.bfloat16)
        picked = jnp.einsum(
            "psrx,mx->psrm", parts, column_hot, preferred_element_type=jnp.float32
        )
        picked = picked[0] + picked[1] + picked[2]
        return jnp.sum(picked * jnp.transpose(row_hot).astype(jnp.float32)[None], axis=1)

    found = lax.map(one_piece, pieces)
    return jnp.moveaxis(found, 1, 0).reshape(species, -1)


def pick_voxels(fields, reached):
    species, planes, columns = fields.shape
    pieces = reached.reshape(-1, SLOT_BLOCK)

    def one_piece(piece):
        row_hot, column_hot = hot_tables(piece, planes, columns)
        picked = jnp.einsum("srx,mx->srm", fields, column_hot, precision=lax.Precision.HIGHEST)
        return jnp.sum(picked * jnp.transpose(row_hot)[None], axis=1)

    found = lax.map(one_piece, pieces)
    return jnp.moveaxis(found, 1, 0).reshape(species, -1)


def spread_voxels(amounts, reached, planes, columns):
    species = amounts.shape[0]
    pieces = reached.reshape(-1, SLOT_BLOCK)
    shares = jnp.moveaxis(amounts.reshape(species, -1, SLOT_BLOCK), 1, 0)

    def add_piece(total, item):
        piece, share = item
        row_hot, column_hot = hot_tables(piece, planes, columns)
        weighted = share[:, :, None] * row_hot[None]
        return (
            total
            + jnp.einsum("smr,mx->srx", weighted, column_hot, precision=lax.Precision.HIGHEST),
            None,
        )

    empty = jnp.zeros((species, planes, columns), jnp.float32)
    total, unused = lax.scan(add_piece, empty, (pieces, shares))
    return total


def force_kernel(chosen_ref, rows_ref, cols_ref, out_ref):
    blocks = out_ref.shape[0]
    picks = chosen_ref.shape[0] // blocks
    chunks = cols_ref.shape[2] // 8
    shape = (8, cols_ref.shape[3])

    def one_block(block, carry):
        own = rows_ref[block + HB]
        mine = [jnp.broadcast_to(own[axis:axis + 1, :], shape) for axis in range(4)]

        def one_pick(pick, totals):
            other = chosen_ref[block * picks + pick]
            totals = list(totals)
            for chunk in range(chunks):
                part = pl.ds(chunk * 8, 8)
                offset = [mine[axis] - cols_ref[other, axis, part, :] for axis in range(3)]
                distance = offset[0] * offset[0] + offset[1] * offset[1] + offset[2] * offset[2]
                strength = REPULSION * jnp.exp(-distance / REPEL_RANGE) - ADHESION * jnp.exp(
                    -distance / ADHERE_RANGE
                )
                weight = mine[3] * cols_ref[other, 3, part, :] * strength
                for axis in range(3):
                    totals[axis] = totals[axis] + offset[axis] * weight
            return tuple(totals)

        zero = jnp.zeros(shape, jnp.float32)
        totals = lax.fori_loop(0, picks, one_pick, (zero, zero, zero))
        out_ref[block] = jnp.concatenate(
            [jnp.sum(total, axis=0, keepdims=True) for total in totals], axis=0
        )
        return carry

    lax.fori_loop(0, blocks, one_block, 0)


def pair_forces(extended, neighbor_blocks):
    coords, span, lanes = extended.shape
    blocks, picks = neighbor_blocks.shape
    rows = jnp.transpose(extended, (1, 0, 2))
    cols = jnp.broadcast_to(rows[:, :, :, None], (span, coords, lanes, lanes))
    pairs = blocks * picks * lanes * lanes
    out = pl.pallas_call(
        force_kernel,
        out_shape=jax.ShapeDtypeStruct((blocks, 3, lanes), jnp.float32),
        in_specs=[
            pl.BlockSpec(memory_space=pltpu.SMEM),
            pl.BlockSpec(memory_space=pltpu.VMEM),
            pl.BlockSpec(memory_space=pltpu.VMEM),
        ],
        out_specs=pl.BlockSpec(memory_space=pltpu.VMEM),
        cost_estimate=pl.CostEstimate(
            flops=26 * pairs, transcendentals=2 * pairs, bytes_accessed=4 * cols.size
        ),
    )(neighbor_blocks.reshape(-1), rows, cols)
    return jnp.transpose(out, (1, 0, 2))


def neighbours(block, axis, dim):
    count = lax.axis_size(axis)
    forward = [(i, i + 1) for i in range(count - 1)]
    backward = [(target, source) for source, target in forward]
    low = lax.ppermute(lax.slice_in_dim(block, block.shape[dim] - 1, None, axis=dim), axis, forward)
    high = lax.ppermute(lax.slice_in_dim(block, 0, 1, axis=dim), axis, backward)
    return (low, high)


def shifted(block, low, high, dim):
    size = block.shape[dim]
    up = jnp.concatenate([lax.slice_in_dim(block, 1, size, axis=dim), high], axis=dim)
    down = jnp.concatenate([low, lax.slice_in_dim(block, 0, size - 1, axis=dim)], axis=dim)
    return (up, down)


def relax_step(center):
    z_low, z_high = neighbours(center, "slab", 1)
    y_low, y_high = neighbours(center, "tile", 2)
    z_up, z_down = shifted(center, z_low, z_high, 1)
    y_up, y_down = shifted(center, y_low, y_high, 2)
    sideways = jnp.pad(center, ((0, 0), (0, 0), (0, 0), (1, 1)))
    beside_all = z_up + z_down
    beside_all = beside_all + y_up + y_down
    beside_all = beside_all + sideways[..., 2:] + sideways[..., :-2]
    spread = jnp.array(DIFFUSION, jnp.float32)[:, None, None, None]
    losses = jnp.array(DECAY, jnp.float32)[:, None, None, None]
    return center + spread * (beside_all - 6.0 * center) - losses * center


def bits_of(width):
    return max(1, (width - 1).bit_length())


def gather_windows(values, starts, length):
    channels, cells = values.shape
    width = cells + length
    rows = starts.shape[0]
    padded = jnp.pad(values, ((0, 0), (0, length)))
    held = jnp.broadcast_to(padded[:, None, :], (channels, rows, width))
    for bit in range(bits_of(width)):
        step = 1 << bit
        take = ((starts >> bit) & 1 == 1)[None, :, None]
        held = jnp.where(take, jnp.roll(held, -step, axis=2), held)
    return held[:, :, :length]


def scatter_windows(windows, starts, cells):
    channels, rows, length = windows.shape
    width = cells + length
    held = jnp.pad(windows, ((0, 0), (0, 0), (0, width - length)))
    for bit in range(bits_of(width)):
        step = 1 << bit
        take = ((starts >> bit) & 1 == 1)[None, :, None]
        held = jnp.where(take, jnp.roll(held, step, axis=2), held)
    return jnp.sum(held[:, :, :cells], axis=1)


def local(
    positions, radius, uptake_rate, voxel_local, cell_counts, send_counts, neighbor_blocks, field
):
    tiles = lax.axis_size("tile")
    capacity = positions.shape[1]
    blocks = capacity // 128
    slot_size = 2 * capacity // tiles
    cell = jnp.arange(capacity, dtype=jnp.int32)
    count = cell_counts[0]
    kept = jnp.where(cell < count, radius, 0.0)
    table = jnp.concatenate([positions, kept[None]], axis=0)
    extended = with_halo(table, (("tile", 1),), HB * 128)
    extended = extended.reshape(4, blocks + 2 * HB, 128)
    forces = pair_forces(extended, neighbor_blocks).reshape(3, capacity)
    sends = send_counts[0]
    ends = jnp.cumsum(sends)
    starts = ends - sends
    ranks = jnp.arange(slot_size, dtype=jnp.int32)
    valid = ranks[None, :] < sends[:, None]
    payload = jnp.stack([voxel_local.astype(jnp.float32), uptake_rate])
    windows = gather_windows(payload, starts, slot_size)
    windows = jnp.where(valid[None], windows, 0.0)
    arrived = lax.all_to_all(windows, "tile", split_axis=1, concat_axis=1, tiled=True)
    forces, arrived = lax.optimization_barrier((forces, arrived))
    reached = arrived[0].reshape(-1).astype(jnp.int32)
    rates = arrived[1].reshape(-1)
    species, depth, rows, columns = field.shape
    planes = depth * rows
    oxygen_rows = field[0].reshape(1, planes, columns)
    oxygen = pick_exact(oxygen_rows, reached, 2 * SLOT_BLOCK)[0]
    consume = rates * oxygen / (MICHAELIS_HALF + oxygen)
    secrete = SECRETION * rates * HYPOXIA_HALF / (HYPOXIA_HALF + oxygen)
    amounts = jnp.stack([-STEP_TIME * consume, STEP_TIME * secrete])
    added = spread_voxels(amounts, reached, planes, columns)
    state = field + added.reshape(species, depth, rows, columns)
    for step in range(ITERS):
        state = relax_step(state)
    vegf = state[1]
    z_low, z_high = neighbours(vegf, "slab", 0)
    y_low, y_high = neighbours(vegf, "tile", 1)
    z_up, z_down = shifted(vegf, z_low, z_high, 0)
    y_up, y_down = shifted(vegf, y_low, y_high, 1)
    rise_z = 0.5 * (z_up - z_down)
    rise_y = 0.5 * (y_up - y_down)
    middle = jnp.pad(vegf, ((0, 0), (0, 0), (1, 1)))
    rise_x = 0.5 * (middle[..., 2:] - middle[..., :-2])
    rises = jnp.stack([rise_z, rise_y, rise_x]).reshape(3, planes, columns)
    slopes = pick_voxels(rises, reached).reshape(3, tiles, slot_size)
    returned = lax.all_to_all(slopes, "tile", split_axis=1, concat_axis=1, tiled=True)
    returned = jnp.where(valid[None], returned, 0.0)
    slope = scatter_windows(returned, starts, capacity)
    velocity = FORCE_SCALE * forces + CHEMOTAXIS * slope
    return (velocity, state)


def solution(mesh):
    placed = (
        P(None, ("slab", "tile")),
        P(("slab", "tile")),
        P(("slab", "tile")),
        P(("slab", "tile")),
        P(("slab", "tile")),
        P(("slab", "tile"), None),
        P(("slab", "tile"), None),
        P(None, "slab", "tile", None),
    )
    return jax.shard_map(
        local,
        mesh=mesh,
        in_specs=placed,
        out_specs=(P(None, ("slab", "tile")), P(None, "slab", "tile", None)),
        check_vma=False,
    )
```

```python
import jax
import jax.numpy as jnp
from jax import lax
from jax.experimental import pallas as pl
from jax.experimental.pallas import tpu as pltpu
from jax.sharding import PartitionSpec as P

HB = 4
K = 8
ITERS = 4


MICHAELIS_HALF = 0.5
HYPOXIA_HALF = 0.6
SECRETION = 0.4
STEP_TIME = 0.5
DIFFUSION = (0.16, 0.12)
DECAY = (0.0, 0.03)
REPULSION = 1.0
ADHESION = 0.35
REPEL_RANGE = 1.0
ADHERE_RANGE = 4.0
FORCE_SCALE = 0.08
CHEMOTAXIS = 1.5
SLOT_BLOCK = 512


def with_halo(block, sides, width):
    for axis, dim in sides:
        count = lax.axis_size(axis)
        forward = [(i, i + 1) for i in range(count - 1)]
        backward = [(target, source) for source, target in forward]
        low = lax.ppermute(
            lax.slice_in_dim(block, block.shape[dim] - width, None, axis=dim), axis, forward
        )
        high = lax.ppermute(lax.slice_in_dim(block, 0, width, axis=dim), axis, backward)
        block = jnp.concatenate([low, block, high], axis=dim)
    return block


def block_force(mine, others):
    offset = mine[:3, :, :, None, None] - others[:3, :, None, :, :]
    distance = jnp.sum(offset * offset, axis=0)
    strength = REPULSION * jnp.exp(-distance / REPEL_RANGE) - ADHESION * jnp.exp(
        -distance / ADHERE_RANGE
    )
    weight = mine[3][:, :, None, None] * others[3][:, None, :, :] * strength
    return jnp.sum(offset * weight[None], axis=(3, 4))


def relax(padded):
    center = padded[:, 1:-1, 1:-1]
    sideways = jnp.pad(center, ((0, 0), (0, 0), (0, 0), (1, 1)))
    beside_all = padded[:, 2:, 1:-1] + padded[:, :-2, 1:-1]
    beside_all = beside_all + padded[:, 1:-1, 2:] + padded[:, 1:-1, :-2]
    beside_all = beside_all + sideways[..., 2:] + sideways[..., :-2]
    spread = jnp.array(DIFFUSION, jnp.float32)[:, None, None, None]
    losses = jnp.array(DECAY, jnp.float32)[:, None, None, None]
    return center + spread * (beside_all - 6.0 * center) - losses * center


def routing(sends, length):
    ends = jnp.cumsum(sends)
    starts = ends - sends
    cell = jnp.arange(length, dtype=jnp.int32)
    target = jnp.sum((ends[:, None] <= cell[None, :]).astype(jnp.int32), axis=0)
    routed = target < sends.shape[0]
    target = jnp.minimum(target, sends.shape[0] - 1)
    lanes = jnp.arange(sends.shape[0], dtype=jnp.int32)
    first = jnp.sum(jnp.where(lanes[:, None] == target[None, :], starts[:, None], 0), axis=0)
    return (target, cell - first, routed)


def hot_tables(piece, planes, columns, kind=jnp.float32):
    row_hot = (piece[:, None] // columns == jnp.arange(planes, dtype=jnp.int32)[None, :]).astype(
        kind
    )
    column_hot = (piece[:, None] % columns == jnp.arange(columns, dtype=jnp.int32)[None, :]).astype(
        kind
    )
    return (row_hot, column_hot)


def split_three(values):
    high = lax.reduce_precision(values, exponent_bits=8, mantissa_bits=7)
    rest = values - high
    middle = lax.reduce_precision(rest, exponent_bits=8, mantissa_bits=7)
    return jnp.stack([high, middle, rest - middle]).astype(jnp.bfloat16)


def pick_exact(fields, reached, block):
    species, planes, columns = fields.shape
    parts = split_three(fields)
    pieces = reached.reshape(-1, block)

    def one_piece(piece):
        row_hot, column_hot = hot_tables(piece, planes, columns, jnp.bfloat16)
        picked = jnp.einsum(
            "psrx,mx->psrm", parts, column_hot, preferred_element_type=jnp.float32
        )
        picked = picked[0] + picked[1] + picked[2]
        return jnp.sum(picked * jnp.transpose(row_hot).astype(jnp.float32)[None], axis=1)

    found = lax.map(one_piece, pieces)
    return jnp.moveaxis(found, 1, 0).reshape(species, -1)


def pick_voxels(fields, reached):
    species, planes, columns = fields.shape
    pieces = reached.reshape(-1, SLOT_BLOCK)

    def one_piece(piece):
        row_hot, column_hot = hot_tables(piece, planes, columns)
        picked = jnp.einsum("srx,mx->srm", fields, column_hot, precision=lax.Precision.HIGHEST)
        return jnp.sum(picked * jnp.transpose(row_hot)[None], axis=1)

    found = lax.map(one_piece, pieces)
    return jnp.moveaxis(found, 1, 0).reshape(species, -1)


def spread_voxels(amounts, reached, planes, columns):
    species = amounts.shape[0]
    pieces = reached.reshape(-1, SLOT_BLOCK)
    shares = jnp.moveaxis(amounts.reshape(species, -1, SLOT_BLOCK), 1, 0)

    def add_piece(total, item):
        piece, share = item
        row_hot, column_hot = hot_tables(piece, planes, columns)
        weighted = share[:, :, None] * row_hot[None]
        return (
            total
            + jnp.einsum("smr,mx->srx", weighted, column_hot, precision=lax.Precision.HIGHEST),
            None,
        )

    empty = jnp.zeros((species, planes, columns), jnp.float32)
    total, unused = lax.scan(add_piece, empty, (pieces, shares))
    return total


def force_kernel(chosen_ref, rows_ref, cols_ref, out_ref):
    blocks = out_ref.shape[0]
    picks = chosen_ref.shape[0] // blocks
    chunks = cols_ref.shape[2] // 8
    shape = (8, cols_ref.shape[3])

    def one_block(block, carry):
        own = rows_ref[block + HB]
        mine = [jnp.broadcast_to(own[axis:axis + 1, :], shape) for axis in range(4)]

        def one_pick(pick, totals):
            other = chosen_ref[block * picks + pick]
            totals = list(totals)
            for chunk in range(chunks):
                part = pl.ds(chunk * 8, 8)
                offset = [mine[axis] - cols_ref[other, axis, part, :] for axis in range(3)]
                distance = offset[0] * offset[0] + offset[1] * offset[1] + offset[2] * offset[2]
                strength = REPULSION * jnp.exp(-distance / REPEL_RANGE) - ADHESION * jnp.exp(
                    -distance / ADHERE_RANGE
                )
                weight = mine[3] * cols_ref[other, 3, part, :] * strength
                for axis in range(3):
                    totals[axis] = totals[axis] + offset[axis] * weight
            return tuple(totals)

        zero = jnp.zeros(shape, jnp.float32)
        totals = lax.fori_loop(0, picks, one_pick, (zero, zero, zero))
        out_ref[block] = jnp.concatenate(
            [jnp.sum(total, axis=0, keepdims=True) for total in totals], axis=0
        )
        return carry

    lax.fori_loop(0, blocks, one_block, 0)


def pair_forces(extended, neighbor_blocks):
    coords, span, lanes = extended.shape
    blocks, picks = neighbor_blocks.shape
    rows = jnp.transpose(extended, (1, 0, 2))
    cols = jnp.broadcast_to(rows[:, :, :, None], (span, coords, lanes, lanes))
    pairs = blocks * picks * lanes * lanes
    out = pl.pallas_call(
        force_kernel,
        out_shape=jax.ShapeDtypeStruct((blocks, 3, lanes), jnp.float32),
        in_specs=[
            pl.BlockSpec(memory_space=pltpu.SMEM),
            pl.BlockSpec(memory_space=pltpu.VMEM),
            pl.BlockSpec(memory_space=pltpu.VMEM),
        ],
        out_specs=pl.BlockSpec(memory_space=pltpu.VMEM),
        cost_estimate=pl.CostEstimate(
            flops=26 * pairs, transcendentals=2 * pairs, bytes_accessed=4 * cols.size
        ),
    )(neighbor_blocks.reshape(-1), rows, cols)
    return jnp.transpose(out, (1, 0, 2))


def neighbours(block, axis, dim):
    count = lax.axis_size(axis)
    forward = [(i, i + 1) for i in range(count - 1)]
    backward = [(target, source) for source, target in forward]
    low = lax.ppermute(lax.slice_in_dim(block, block.shape[dim] - 1, None, axis=dim), axis, forward)
    high = lax.ppermute(lax.slice_in_dim(block, 0, 1, axis=dim), axis, backward)
    return (low, high)


def shifted(block, low, high, dim):
    size = block.shape[dim]
    up = jnp.concatenate([lax.slice_in_dim(block, 1, size, axis=dim), high], axis=dim)
    down = jnp.concatenate([low, lax.slice_in_dim(block, 0, size - 1, axis=dim)], axis=dim)
    return (up, down)


def relax_step(center):
    z_low, z_high = neighbours(center, "slab", 1)
    y_low, y_high = neighbours(center, "tile", 2)
    z_up, z_down = shifted(center, z_low, z_high, 1)
    y_up, y_down = shifted(center, y_low, y_high, 2)
    sideways = jnp.pad(center, ((0, 0), (0, 0), (0, 0), (1, 1)))
    beside_all = z_up + z_down
    beside_all = beside_all + y_up + y_down
    beside_all = beside_all + sideways[..., 2:] + sideways[..., :-2]
    spread = jnp.array(DIFFUSION, jnp.float32)[:, None, None, None]
    losses = jnp.array(DECAY, jnp.float32)[:, None, None, None]
    return center + spread * (beside_all - 6.0 * center) - losses * center


def bits_of(width):
    return max(1, (width - 1).bit_length())


def gather_windows(values, starts, length):
    channels, cells = values.shape
    width = cells + length
    rows = starts.shape[0]
    padded = jnp.pad(values, ((0, 0), (0, length)))
    held = jnp.broadcast_to(padded[:, None, :], (channels, rows, width))
    for bit in range(bits_of(width)):
        step = 1 << bit
        take = ((starts >> bit) & 1 == 1)[None, :, None]
        held = jnp.where(take, jnp.roll(held, -step, axis=2), held)
    return held[:, :, :length]


def scatter_windows(windows, starts, cells):
    channels, rows, length = windows.shape
    width = cells + length
    held = jnp.pad(windows, ((0, 0), (0, 0), (0, width - length)))
    for bit in range(bits_of(width)):
        step = 1 << bit
        take = ((starts >> bit) & 1 == 1)[None, :, None]
        held = jnp.where(take, jnp.roll(held, step, axis=2), held)
    return jnp.sum(held[:, :, :cells], axis=1)


def local(
    positions, radius, uptake_rate, voxel_local, cell_counts, send_counts, neighbor_blocks, field
):
    tiles = lax.axis_size("tile")
    capacity = positions.shape[1]
    blocks = capacity // 128
    slot_size = 2 * capacity // tiles
    cell = jnp.arange(capacity, dtype=jnp.int32)
    count = cell_counts[0]
    kept = jnp.where(cell < count, radius, 0.0)
    table = jnp.concatenate([positions, kept[None]], axis=0)
    extended = with_halo(table, (("tile", 1),), HB * 128)
    extended = extended.reshape(4, blocks + 2 * HB, 128)
    forces = pair_forces(extended, neighbor_blocks).reshape(3, capacity)
    sends = send_counts[0]
    ends = jnp.cumsum(sends)
    starts = ends - sends
    ranks = jnp.arange(slot_size, dtype=jnp.int32)
    valid = ranks[None, :] < sends[:, None]
    payload = jnp.stack([voxel_local.astype(jnp.float32), uptake_rate])
    windows = gather_windows(payload, starts, slot_size)
    windows = jnp.where(valid[None], windows, 0.0)
    arrived = lax.all_to_all(windows, "tile", split_axis=1, concat_axis=1, tiled=True)
    reached = arrived[0].reshape(-1).astype(jnp.int32)
    rates = arrived[1].reshape(-1)
    species, depth, rows, columns = field.shape
    planes = depth * rows
    oxygen_rows = field[0].reshape(1, planes, columns)
    oxygen = pick_exact(oxygen_rows, reached, 2 * SLOT_BLOCK)[0]
    consume = rates * oxygen / (MICHAELIS_HALF + oxygen)
    secrete = SECRETION * rates * HYPOXIA_HALF / (HYPOXIA_HALF + oxygen)
    amounts = jnp.stack([-STEP_TIME * consume, STEP_TIME * secrete])
    added = spread_voxels(amounts, reached, planes, columns)
    state = field + added.reshape(species, depth, rows, columns)
    for step in range(ITERS):
        state = relax_step(state)
    vegf = state[1]
    z_low, z_high = neighbours(vegf, "slab", 0)
    y_low, y_high = neighbours(vegf, "tile", 1)
    z_up, z_down = shifted(vegf, z_low, z_high, 0)
    y_up, y_down = shifted(vegf, y_low, y_high, 1)
    rise_z = 0.5 * (z_up - z_down)
    rise_y = 0.5 * (y_up - y_down)
    middle = jnp.pad(vegf, ((0, 0), (0, 0), (1, 1)))
    rise_x = 0.5 * (middle[..., 2:] - middle[..., :-2])
    rises = jnp.stack([rise_z, rise_y, rise_x]).reshape(3, planes, columns)
    slopes = pick_voxels(rises, reached).reshape(3, tiles, slot_size)
    returned = lax.all_to_all(slopes, "tile", split_axis=1, concat_axis=1, tiled=True)
    returned = jnp.where(valid[None], returned, 0.0)
    slope = scatter_windows(returned, starts, capacity)
    velocity = FORCE_SCALE * forces + CHEMOTAXIS * slope
    return (velocity, state)


def solution(mesh):
    placed = (
        P(None, ("slab", "tile")),
        P(("slab", "tile")),
        P(("slab", "tile")),
        P(("slab", "tile")),
        P(("slab", "tile")),
        P(("slab", "tile"), None),
        P(("slab", "tile"), None),
        P(None, "slab", "tile", None),
    )
    return jax.shard_map(
        local,
        mesh=mesh,
        in_specs=placed,
        out_specs=(P(None, ("slab", "tile")), P(None, "slab", "tile", None)),
        check_vma=False,
    )
```

```python
import jax
import jax.numpy as jnp
from jax import lax
from jax.experimental import pallas as pl
from jax.experimental.pallas import tpu as pltpu
from jax.sharding import PartitionSpec as P

HB = 4
K = 8
ITERS = 4


MICHAELIS_HALF = 0.5
HYPOXIA_HALF = 0.6
SECRETION = 0.4
STEP_TIME = 0.5
DIFFUSION = (0.16, 0.12)
DECAY = (0.0, 0.03)
REPULSION = 1.0
ADHESION = 0.35
REPEL_RANGE = 1.0
ADHERE_RANGE = 4.0
FORCE_SCALE = 0.08
CHEMOTAXIS = 1.5
SLOT_BLOCK = 512


def with_halo(block, sides, width):
    for axis, dim in sides:
        count = lax.axis_size(axis)
        forward = [(i, i + 1) for i in range(count - 1)]
        backward = [(target, source) for source, target in forward]
        low = lax.ppermute(
            lax.slice_in_dim(block, block.shape[dim] - width, None, axis=dim), axis, forward
        )
        high = lax.ppermute(lax.slice_in_dim(block, 0, width, axis=dim), axis, backward)
        block = jnp.concatenate([low, block, high], axis=dim)
    return block


def block_force(mine, others):
    offset = mine[:3, :, :, None, None] - others[:3, :, None, :, :]
    distance = jnp.sum(offset * offset, axis=0)
    strength = REPULSION * jnp.exp(-distance / REPEL_RANGE) - ADHESION * jnp.exp(
        -distance / ADHERE_RANGE
    )
    weight = mine[3][:, :, None, None] * others[3][:, None, :, :] * strength
    return jnp.sum(offset * weight[None], axis=(3, 4))


def relax(padded):
    center = padded[:, 1:-1, 1:-1]
    sideways = jnp.pad(center, ((0, 0), (0, 0), (0, 0), (1, 1)))
    beside_all = padded[:, 2:, 1:-1] + padded[:, :-2, 1:-1]
    beside_all = beside_all + padded[:, 1:-1, 2:] + padded[:, 1:-1, :-2]
    beside_all = beside_all + sideways[..., 2:] + sideways[..., :-2]
    spread = jnp.array(DIFFUSION, jnp.float32)[:, None, None, None]
    losses = jnp.array(DECAY, jnp.float32)[:, None, None, None]
    return center + spread * (beside_all - 6.0 * center) - losses * center


def routing(sends, length):
    ends = jnp.cumsum(sends)
    starts = ends - sends
    cell = jnp.arange(length, dtype=jnp.int32)
    target = jnp.sum((ends[:, None] <= cell[None, :]).astype(jnp.int32), axis=0)
    routed = target < sends.shape[0]
    target = jnp.minimum(target, sends.shape[0] - 1)
    lanes = jnp.arange(sends.shape[0], dtype=jnp.int32)
    first = jnp.sum(jnp.where(lanes[:, None] == target[None, :], starts[:, None], 0), axis=0)
    return (target, cell - first, routed)


def hot_tables(piece, planes, columns, kind=jnp.float32):
    row_hot = (piece[:, None] // columns == jnp.arange(planes, dtype=jnp.int32)[None, :]).astype(
        kind
    )
    column_hot = (piece[:, None] % columns == jnp.arange(columns, dtype=jnp.int32)[None, :]).astype(
        kind
    )
    return (row_hot, column_hot)


def split_three(values):
    high = lax.reduce_precision(values, exponent_bits=8, mantissa_bits=7)
    rest = values - high
    middle = lax.reduce_precision(rest, exponent_bits=8, mantissa_bits=7)
    return jnp.stack([high, middle, rest - middle]).astype(jnp.bfloat16)


def pick_exact(fields, reached, block):
    species, planes, columns = fields.shape
    parts = split_three(fields)
    pieces = reached.reshape(-1, block)

    def one_piece(piece):
        row_hot, column_hot = hot_tables(piece, planes, columns, jnp.bfloat16)
        picked = jnp.einsum(
            "psrx,mx->psrm", parts, column_hot, preferred_element_type=jnp.float32
        )
        picked = picked[0] + picked[1] + picked[2]
        return jnp.sum(picked * jnp.transpose(row_hot).astype(jnp.float32)[None], axis=1)

    found = lax.map(one_piece, pieces)
    return jnp.moveaxis(found, 1, 0).reshape(species, -1)


def pick_voxels(fields, reached):
    species, planes, columns = fields.shape
    pieces = reached.reshape(-1, SLOT_BLOCK)

    def one_piece(piece):
        row_hot, column_hot = hot_tables(piece, planes, columns)
        picked = jnp.einsum("srx,mx->srm", fields, column_hot, precision=lax.Precision.HIGHEST)
        return jnp.sum(picked * jnp.transpose(row_hot)[None], axis=1)

    found = lax.map(one_piece, pieces)
    return jnp.moveaxis(found, 1, 0).reshape(species, -1)


def spread_voxels(amounts, reached, planes, columns):
    species = amounts.shape[0]
    pieces = reached.reshape(-1, SLOT_BLOCK)
    shares = jnp.moveaxis(amounts.reshape(species, -1, SLOT_BLOCK), 1, 0)

    def add_piece(total, item):
        piece, share = item
        row_hot, column_hot = hot_tables(piece, planes, columns)
        weighted = share[:, :, None] * row_hot[None]
        return (
            total
            + jnp.einsum("smr,mx->srx", weighted, column_hot, precision=lax.Precision.HIGHEST),
            None,
        )

    empty = jnp.zeros((species, planes, columns), jnp.float32)
    total, unused = lax.scan(add_piece, empty, (pieces, shares))
    return total


def force_kernel(chosen_ref, rows_ref, cols_ref, out_ref):
    blocks = out_ref.shape[0]
    picks = chosen_ref.shape[0] // blocks
    chunks = cols_ref.shape[2] // 8
    shape = (8, cols_ref.shape[3])

    def one_block(block, carry):
        own = rows_ref[block + HB]
        mine = [jnp.broadcast_to(own[axis:axis + 1, :], shape) for axis in range(4)]

        def one_pick(pick, totals):
            other = chosen_ref[block * picks + pick]
            totals = list(totals)
            for chunk in range(chunks):
                part = pl.ds(chunk * 8, 8)
                offset = [mine[axis] - cols_ref[other, axis, part, :] for axis in range(3)]
                distance = offset[0] * offset[0] + offset[1] * offset[1] + offset[2] * offset[2]
                strength = REPULSION * jnp.exp(-distance / REPEL_RANGE) - ADHESION * jnp.exp(
                    -distance / ADHERE_RANGE
                )
                weight = mine[3] * cols_ref[other, 3, part, :] * strength
                for axis in range(3):
                    totals[axis] = totals[axis] + offset[axis] * weight
            return tuple(totals)

        zero = jnp.zeros(shape, jnp.float32)
        totals = lax.fori_loop(0, picks, one_pick, (zero, zero, zero))
        out_ref[block] = jnp.concatenate(
            [jnp.sum(total, axis=0, keepdims=True) for total in totals], axis=0
        )
        return carry

    lax.fori_loop(0, blocks, one_block, 0)


def pair_forces(extended, neighbor_blocks):
    coords, span, lanes = extended.shape
    blocks, picks = neighbor_blocks.shape
    rows = jnp.transpose(extended, (1, 0, 2))
    cols = jnp.broadcast_to(rows[:, :, :, None], (span, coords, lanes, lanes))
    pairs = blocks * picks * lanes * lanes
    out = pl.pallas_call(
        force_kernel,
        out_shape=jax.ShapeDtypeStruct((blocks, 3, lanes), jnp.float32),
        in_specs=[
            pl.BlockSpec(memory_space=pltpu.SMEM),
            pl.BlockSpec(memory_space=pltpu.VMEM),
            pl.BlockSpec(memory_space=pltpu.VMEM),
        ],
        out_specs=pl.BlockSpec(memory_space=pltpu.VMEM),
        cost_estimate=pl.CostEstimate(
            flops=26 * pairs, transcendentals=2 * pairs, bytes_accessed=4 * cols.size
        ),
    )(neighbor_blocks.reshape(-1), rows, cols)
    return jnp.transpose(out, (1, 0, 2))


def deep_halo(block, axis, dim, width):
    count = lax.axis_size(axis)
    forward = [(i, i + 1) for i in range(count - 1)]
    backward = [(target, source) for source, target in forward]
    size = block.shape[dim]
    low = lax.ppermute(lax.slice_in_dim(block, size - width, None, axis=dim), axis, forward)
    high = lax.ppermute(lax.slice_in_dim(block, 0, width, axis=dim), axis, backward)
    return jnp.concatenate([low, block, high], axis=dim)


def neighbours(block, axis, dim):
    count = lax.axis_size(axis)
    forward = [(i, i + 1) for i in range(count - 1)]
    backward = [(target, source) for source, target in forward]
    low = lax.ppermute(lax.slice_in_dim(block, block.shape[dim] - 1, None, axis=dim), axis, forward)
    high = lax.ppermute(lax.slice_in_dim(block, 0, 1, axis=dim), axis, backward)
    return (low, high)


def shifted(block, low, high, dim):
    size = block.shape[dim]
    up = jnp.concatenate([lax.slice_in_dim(block, 1, size, axis=dim), high], axis=dim)
    down = jnp.concatenate([low, lax.slice_in_dim(block, 0, size - 1, axis=dim)], axis=dim)
    return (up, down)


def relax_step(center):
    z_low, z_high = neighbours(center, "slab", 1)
    y_low, y_high = neighbours(center, "tile", 2)
    z_up, z_down = shifted(center, z_low, z_high, 1)
    y_up, y_down = shifted(center, y_low, y_high, 2)
    sideways = jnp.pad(center, ((0, 0), (0, 0), (0, 0), (1, 1)))
    beside_all = z_up + z_down
    beside_all = beside_all + y_up + y_down
    beside_all = beside_all + sideways[..., 2:] + sideways[..., :-2]
    spread = jnp.array(DIFFUSION, jnp.float32)[:, None, None, None]
    losses = jnp.array(DECAY, jnp.float32)[:, None, None, None]
    return center + spread * (beside_all - 6.0 * center) - losses * center


def bits_of(width):
    return max(1, (width - 1).bit_length())


def gather_windows(values, starts, length):
    channels, cells = values.shape
    width = cells + length
    rows = starts.shape[0]
    padded = jnp.pad(values, ((0, 0), (0, length)))
    held = jnp.broadcast_to(padded[:, None, :], (channels, rows, width))
    for bit in range(bits_of(width)):
        step = 1 << bit
        take = ((starts >> bit) & 1 == 1)[None, :, None]
        held = jnp.where(take, jnp.roll(held, -step, axis=2), held)
    return held[:, :, :length]


def scatter_windows(windows, starts, cells):
    channels, rows, length = windows.shape
    width = cells + length
    held = jnp.pad(windows, ((0, 0), (0, 0), (0, width - length)))
    for bit in range(bits_of(width)):
        step = 1 << bit
        take = ((starts >> bit) & 1 == 1)[None, :, None]
        held = jnp.where(take, jnp.roll(held, step, axis=2), held)
    return jnp.sum(held[:, :, :cells], axis=1)


def local(
    positions, radius, uptake_rate, voxel_local, cell_counts, send_counts, neighbor_blocks, field
):
    tiles = lax.axis_size("tile")
    capacity = positions.shape[1]
    blocks = capacity // 128
    slot_size = 2 * capacity // tiles
    cell = jnp.arange(capacity, dtype=jnp.int32)
    count = cell_counts[0]
    kept = jnp.where(cell < count, radius, 0.0)
    table = jnp.concatenate([positions, kept[None]], axis=0)
    extended = with_halo(table, (("tile", 1),), HB * 128)
    extended = extended.reshape(4, blocks + 2 * HB, 128)
    forces = pair_forces(extended, neighbor_blocks).reshape(3, capacity)
    sends = send_counts[0]
    ends = jnp.cumsum(sends)
    starts = ends - sends
    ranks = jnp.arange(slot_size, dtype=jnp.int32)
    valid = ranks[None, :] < sends[:, None]
    payload = jnp.stack([voxel_local.astype(jnp.float32), uptake_rate])
    windows = gather_windows(payload, starts, slot_size)
    windows = jnp.where(valid[None], windows, 0.0)
    arrived = lax.all_to_all(windows, "tile", split_axis=1, concat_axis=1, tiled=True)
    reached = arrived[0].reshape(-1).astype(jnp.int32)
    rates = arrived[1].reshape(-1)
    species, depth, rows, columns = field.shape
    planes = depth * rows
    oxygen_rows = field[0].reshape(1, planes, columns)
    oxygen = pick_exact(oxygen_rows, reached, 2 * SLOT_BLOCK)[0]
    consume = rates * oxygen / (MICHAELIS_HALF + oxygen)
    secrete = SECRETION * rates * HYPOXIA_HALF / (HYPOXIA_HALF + oxygen)
    amounts = jnp.stack([-STEP_TIME * consume, STEP_TIME * secrete])
    added = spread_voxels(amounts, reached, planes, columns)
    state = field + added.reshape(species, depth, rows, columns)
    depth_of, rows_of = depth, rows
    halo = ITERS + 1
    ext = deep_halo(state, "slab", 1, halo)
    ext = deep_halo(ext, "tile", 2, halo)
    first_plane = lax.axis_index("slab") * depth_of
    first_row = lax.axis_index("tile") * rows_of
    all_planes = lax.axis_size("slab") * depth_of
    all_rows = lax.axis_size("tile") * rows_of
    for step in range(ITERS):
        ext = relax(ext)
        left = halo - step - 1
        plane = first_plane - left + jnp.arange(ext.shape[1], dtype=jnp.int32)
        row = first_row - left + jnp.arange(ext.shape[2], dtype=jnp.int32)
        inside = ((plane >= 0) & (plane < all_planes))[:, None] & ((row >= 0) & (row < all_rows))[None, :]
        ext = jnp.where(inside[None, :, :, None], ext, 0.0)
    state = ext[:, 1:-1, 1:-1]
    border = ext[1]
    rise_z = 0.5 * (border[2:, 1:-1] - border[:-2, 1:-1])
    rise_y = 0.5 * (border[1:-1, 2:] - border[1:-1, :-2])
    middle = jnp.pad(border[1:-1, 1:-1], ((0, 0), (0, 0), (1, 1)))
    rise_x = 0.5 * (middle[..., 2:] - middle[..., :-2])
    rises = jnp.stack([rise_z, rise_y, rise_x]).reshape(3, planes, columns)
    slopes = pick_voxels(rises, reached).reshape(3, tiles, slot_size)
    returned = lax.all_to_all(slopes, "tile", split_axis=1, concat_axis=1, tiled=True)
    returned = jnp.where(valid[None], returned, 0.0)
    slope = scatter_windows(returned, starts, capacity)
    velocity = FORCE_SCALE * forces + CHEMOTAXIS * slope
    return (velocity, state)


def solution(mesh):
    placed = (
        P(None, ("slab", "tile")),
        P(("slab", "tile")),
        P(("slab", "tile")),
        P(("slab", "tile")),
        P(("slab", "tile")),
        P(("slab", "tile"), None),
        P(("slab", "tile"), None),
        P(None, "slab", "tile", None),
    )
    return jax.shard_map(
        local,
        mesh=mesh,
        in_specs=placed,
        out_specs=(P(None, ("slab", "tile")), P(None, "slab", "tile", None)),
        check_vma=False,
    )
```

```python
import jax
import jax.numpy as jnp
from jax import lax
from jax.experimental import pallas as pl
from jax.experimental.pallas import tpu as pltpu
from jax.sharding import PartitionSpec as P

HB = 4
K = 8
ITERS = 4


MICHAELIS_HALF = 0.5
HYPOXIA_HALF = 0.6
SECRETION = 0.4
STEP_TIME = 0.5
DIFFUSION = (0.16, 0.12)
DECAY = (0.0, 0.03)
REPULSION = 1.0
ADHESION = 0.35
REPEL_RANGE = 1.0
ADHERE_RANGE = 4.0
FORCE_SCALE = 0.08
CHEMOTAXIS = 1.5
SLOT_BLOCK = 512


def with_halo(block, sides, width):
    for axis, dim in sides:
        count = lax.axis_size(axis)
        forward = [(i, i + 1) for i in range(count - 1)]
        backward = [(target, source) for source, target in forward]
        low = lax.ppermute(
            lax.slice_in_dim(block, block.shape[dim] - width, None, axis=dim), axis, forward
        )
        high = lax.ppermute(lax.slice_in_dim(block, 0, width, axis=dim), axis, backward)
        block = jnp.concatenate([low, block, high], axis=dim)
    return block


def block_force(mine, others):
    offset = mine[:3, :, :, None, None] - others[:3, :, None, :, :]
    distance = jnp.sum(offset * offset, axis=0)
    strength = REPULSION * jnp.exp(-distance / REPEL_RANGE) - ADHESION * jnp.exp(
        -distance / ADHERE_RANGE
    )
    weight = mine[3][:, :, None, None] * others[3][:, None, :, :] * strength
    return jnp.sum(offset * weight[None], axis=(3, 4))


def relax(padded):
    center = padded[:, 1:-1, 1:-1]
    sideways = jnp.pad(center, ((0, 0), (0, 0), (0, 0), (1, 1)))
    beside_all = padded[:, 2:, 1:-1] + padded[:, :-2, 1:-1]
    beside_all = beside_all + padded[:, 1:-1, 2:] + padded[:, 1:-1, :-2]
    beside_all = beside_all + sideways[..., 2:] + sideways[..., :-2]
    spread = jnp.array(DIFFUSION, jnp.float32)[:, None, None, None]
    losses = jnp.array(DECAY, jnp.float32)[:, None, None, None]
    return center + spread * (beside_all - 6.0 * center) - losses * center


def routing(sends, length):
    ends = jnp.cumsum(sends)
    starts = ends - sends
    cell = jnp.arange(length, dtype=jnp.int32)
    target = jnp.sum((ends[:, None] <= cell[None, :]).astype(jnp.int32), axis=0)
    routed = target < sends.shape[0]
    target = jnp.minimum(target, sends.shape[0] - 1)
    lanes = jnp.arange(sends.shape[0], dtype=jnp.int32)
    first = jnp.sum(jnp.where(lanes[:, None] == target[None, :], starts[:, None], 0), axis=0)
    return (target, cell - first, routed)


def hot_tables(piece, planes, columns, kind=jnp.float32):
    row_hot = (piece[:, None] // columns == jnp.arange(planes, dtype=jnp.int32)[None, :]).astype(
        kind
    )
    column_hot = (piece[:, None] % columns == jnp.arange(columns, dtype=jnp.int32)[None, :]).astype(
        kind
    )
    return (row_hot, column_hot)


def split_three(values):
    high = lax.reduce_precision(values, exponent_bits=8, mantissa_bits=7)
    rest = values - high
    middle = lax.reduce_precision(rest, exponent_bits=8, mantissa_bits=7)
    return jnp.stack([high, middle, rest - middle]).astype(jnp.bfloat16)


def pick_exact(fields, reached, block):
    species, planes, columns = fields.shape
    parts = split_three(fields)
    pieces = reached.reshape(-1, block)

    def one_piece(piece):
        row_hot, column_hot = hot_tables(piece, planes, columns, jnp.bfloat16)
        picked = jnp.einsum(
            "psrx,mx->psrm", parts, column_hot, preferred_element_type=jnp.float32
        )
        picked = picked[0] + picked[1] + picked[2]
        return jnp.sum(picked * jnp.transpose(row_hot).astype(jnp.float32)[None], axis=1)

    found = lax.map(one_piece, pieces)
    return jnp.moveaxis(found, 1, 0).reshape(species, -1)


def pick_voxels(fields, reached):
    species, planes, columns = fields.shape
    pieces = reached.reshape(-1, SLOT_BLOCK)

    def one_piece(piece):
        row_hot, column_hot = hot_tables(piece, planes, columns)
        picked = jnp.einsum("srx,mx->srm", fields, column_hot, precision=lax.Precision.HIGHEST)
        return jnp.sum(picked * jnp.transpose(row_hot)[None], axis=1)

    found = lax.map(one_piece, pieces)
    return jnp.moveaxis(found, 1, 0).reshape(species, -1)


def spread_voxels(amounts, reached, planes, columns):
    species = amounts.shape[0]
    pieces = reached.reshape(-1, SLOT_BLOCK)
    shares = jnp.moveaxis(amounts.reshape(species, -1, SLOT_BLOCK), 1, 0)

    def add_piece(total, item):
        piece, share = item
        row_hot, column_hot = hot_tables(piece, planes, columns)
        weighted = share[:, :, None] * row_hot[None]
        return (
            total
            + jnp.einsum("smr,mx->srx", weighted, column_hot, precision=lax.Precision.HIGHEST),
            None,
        )

    empty = jnp.zeros((species, planes, columns), jnp.float32)
    total, unused = lax.scan(add_piece, empty, (pieces, shares))
    return total


def force_kernel(chosen_ref, rows_ref, cols_ref, out_ref):
    blocks = out_ref.shape[0]
    picks = chosen_ref.shape[0] // blocks
    chunks = cols_ref.shape[2] // 8
    shape = (8, cols_ref.shape[3])

    def one_block(block, carry):
        own = rows_ref[block + HB]
        mine = [jnp.broadcast_to(own[axis:axis + 1, :], shape) for axis in range(4)]

        def one_pick(pick, totals):
            other = chosen_ref[block * picks + pick]
            totals = list(totals)
            for chunk in range(chunks):
                part = pl.ds(chunk * 8, 8)
                offset = [mine[axis] - cols_ref[other, axis, part, :] for axis in range(3)]
                distance = offset[0] * offset[0] + offset[1] * offset[1] + offset[2] * offset[2]
                strength = REPULSION * jnp.exp(-distance / REPEL_RANGE) - ADHESION * jnp.exp(
                    -distance / ADHERE_RANGE
                )
                weight = mine[3] * cols_ref[other, 3, part, :] * strength
                for axis in range(3):
                    totals[axis] = totals[axis] + offset[axis] * weight
            return tuple(totals)

        zero = jnp.zeros(shape, jnp.float32)
        totals = lax.fori_loop(0, picks, one_pick, (zero, zero, zero))
        out_ref[block] = jnp.concatenate(
            [jnp.sum(total, axis=0, keepdims=True) for total in totals], axis=0
        )
        return carry

    lax.fori_loop(0, blocks, one_block, 0)


def pair_forces(extended, neighbor_blocks):
    coords, span, lanes = extended.shape
    blocks, picks = neighbor_blocks.shape
    rows = jnp.transpose(extended, (1, 0, 2))
    cols = jnp.broadcast_to(rows[:, :, :, None], (span, coords, lanes, lanes))
    pairs = blocks * picks * lanes * lanes
    out = pl.pallas_call(
        force_kernel,
        out_shape=jax.ShapeDtypeStruct((blocks, 3, lanes), jnp.float32),
        in_specs=[
            pl.BlockSpec(memory_space=pltpu.SMEM),
            pl.BlockSpec(memory_space=pltpu.VMEM),
            pl.BlockSpec(memory_space=pltpu.VMEM),
        ],
        out_specs=pl.BlockSpec(memory_space=pltpu.VMEM),
        cost_estimate=pl.CostEstimate(
            flops=26 * pairs, transcendentals=2 * pairs, bytes_accessed=4 * cols.size
        ),
    )(neighbor_blocks.reshape(-1), rows, cols)
    return jnp.transpose(out, (1, 0, 2))


def deposit_voxels(oxygen_rows, reached, rates, planes, columns):
    pieces = reached.reshape(-1, SLOT_BLOCK)
    shares = rates.reshape(-1, SLOT_BLOCK)

    def add_piece(total, item):
        piece, rate = item
        row_hot, column_hot = hot_tables(piece, planes, columns)
        picked = jnp.einsum(
            "srx,mx->srm", oxygen_rows, column_hot, precision=lax.Precision.HIGHEST
        )
        oxygen = jnp.sum(picked * jnp.transpose(row_hot)[None], axis=1)[0]
        consume = rate * oxygen / (MICHAELIS_HALF + oxygen)
        secrete = SECRETION * rate * HYPOXIA_HALF / (HYPOXIA_HALF + oxygen)
        share = jnp.stack([-STEP_TIME * consume, STEP_TIME * secrete])
        weighted = share[:, :, None] * row_hot[None]
        return (
            total
            + jnp.einsum("smr,mx->srx", weighted, column_hot, precision=lax.Precision.HIGHEST),
            None,
        )

    empty = jnp.zeros((2, planes, columns), jnp.float32)
    total, unused = lax.scan(add_piece, empty, (pieces, shares))
    return total


def neighbours(block, axis, dim):
    count = lax.axis_size(axis)
    forward = [(i, i + 1) for i in range(count - 1)]
    backward = [(target, source) for source, target in forward]
    low = lax.ppermute(lax.slice_in_dim(block, block.shape[dim] - 1, None, axis=dim), axis, forward)
    high = lax.ppermute(lax.slice_in_dim(block, 0, 1, axis=dim), axis, backward)
    return (low, high)


def shifted(block, low, high, dim):
    size = block.shape[dim]
    up = jnp.concatenate([lax.slice_in_dim(block, 1, size, axis=dim), high], axis=dim)
    down = jnp.concatenate([low, lax.slice_in_dim(block, 0, size - 1, axis=dim)], axis=dim)
    return (up, down)


def relax_step(center):
    z_low, z_high = neighbours(center, "slab", 1)
    y_low, y_high = neighbours(center, "tile", 2)
    z_up, z_down = shifted(center, z_low, z_high, 1)
    y_up, y_down = shifted(center, y_low, y_high, 2)
    sideways = jnp.pad(center, ((0, 0), (0, 0), (0, 0), (1, 1)))
    beside_all = z_up + z_down
    beside_all = beside_all + y_up + y_down
    beside_all = beside_all + sideways[..., 2:] + sideways[..., :-2]
    spread = jnp.array(DIFFUSION, jnp.float32)[:, None, None, None]
    losses = jnp.array(DECAY, jnp.float32)[:, None, None, None]
    return center + spread * (beside_all - 6.0 * center) - losses * center


def bits_of(width):
    return max(1, (width - 1).bit_length())


def gather_windows(values, starts, length):
    channels, cells = values.shape
    width = cells + length
    rows = starts.shape[0]
    padded = jnp.pad(values, ((0, 0), (0, length)))
    held = jnp.broadcast_to(padded[:, None, :], (channels, rows, width))
    for bit in range(bits_of(width)):
        step = 1 << bit
        take = ((starts >> bit) & 1 == 1)[None, :, None]
        held = jnp.where(take, jnp.roll(held, -step, axis=2), held)
    return held[:, :, :length]


def scatter_windows(windows, starts, cells):
    channels, rows, length = windows.shape
    width = cells + length
    held = jnp.pad(windows, ((0, 0), (0, 0), (0, width - length)))
    for bit in range(bits_of(width)):
        step = 1 << bit
        take = ((starts >> bit) & 1 == 1)[None, :, None]
        held = jnp.where(take, jnp.roll(held, step, axis=2), held)
    return jnp.sum(held[:, :, :cells], axis=1)


def local(
    positions, radius, uptake_rate, voxel_local, cell_counts, send_counts, neighbor_blocks, field
):
    tiles = lax.axis_size("tile")
    capacity = positions.shape[1]
    blocks = capacity // 128
    slot_size = 2 * capacity // tiles
    cell = jnp.arange(capacity, dtype=jnp.int32)
    count = cell_counts[0]
    kept = jnp.where(cell < count, radius, 0.0)
    table = jnp.concatenate([positions, kept[None]], axis=0)
    extended = with_halo(table, (("tile", 1),), HB * 128)
    extended = extended.reshape(4, blocks + 2 * HB, 128)
    forces = pair_forces(extended, neighbor_blocks).reshape(3, capacity)
    sends = send_counts[0]
    ends = jnp.cumsum(sends)
    starts = ends - sends
    ranks = jnp.arange(slot_size, dtype=jnp.int32)
    valid = ranks[None, :] < sends[:, None]
    payload = jnp.stack([voxel_local.astype(jnp.float32), uptake_rate])
    windows = gather_windows(payload, starts, slot_size)
    windows = jnp.where(valid[None], windows, 0.0)
    arrived = lax.all_to_all(windows, "tile", split_axis=1, concat_axis=1, tiled=True)
    reached = arrived[0].reshape(-1).astype(jnp.int32)
    rates = arrived[1].reshape(-1)
    species, depth, rows, columns = field.shape
    planes = depth * rows
    oxygen_rows = field[0].reshape(1, planes, columns)
    added = deposit_voxels(oxygen_rows, reached, rates, planes, columns)
    state = field + added.reshape(species, depth, rows, columns)
    for step in range(ITERS):
        state = relax_step(state)
    vegf = state[1]
    z_low, z_high = neighbours(vegf, "slab", 0)
    y_low, y_high = neighbours(vegf, "tile", 1)
    z_up, z_down = shifted(vegf, z_low, z_high, 0)
    y_up, y_down = shifted(vegf, y_low, y_high, 1)
    rise_z = 0.5 * (z_up - z_down)
    rise_y = 0.5 * (y_up - y_down)
    middle = jnp.pad(vegf, ((0, 0), (0, 0), (1, 1)))
    rise_x = 0.5 * (middle[..., 2:] - middle[..., :-2])
    rises = jnp.stack([rise_z, rise_y, rise_x]).reshape(3, planes, columns)
    slopes = pick_voxels(rises, reached).reshape(3, tiles, slot_size)
    returned = lax.all_to_all(slopes, "tile", split_axis=1, concat_axis=1, tiled=True)
    returned = jnp.where(valid[None], returned, 0.0)
    slope = scatter_windows(returned, starts, capacity)
    velocity = FORCE_SCALE * forces + CHEMOTAXIS * slope
    return (velocity, state)


def solution(mesh):
    placed = (
        P(None, ("slab", "tile")),
        P(("slab", "tile")),
        P(("slab", "tile")),
        P(("slab", "tile")),
        P(("slab", "tile")),
        P(("slab", "tile"), None),
        P(("slab", "tile"), None),
        P(None, "slab", "tile", None),
    )
    return jax.shard_map(
        local,
        mesh=mesh,
        in_specs=placed,
        out_specs=(P(None, ("slab", "tile")), P(None, "slab", "tile", None)),
        check_vma=False,
    )
```

```python
import jax
import jax.numpy as jnp
from jax import lax
from jax.experimental import pallas as pl
from jax.experimental.pallas import tpu as pltpu
from jax.sharding import PartitionSpec as P

HB = 4
K = 8
ITERS = 4


MICHAELIS_HALF = 0.5
HYPOXIA_HALF = 0.6
SECRETION = 0.4
STEP_TIME = 0.5
DIFFUSION = (0.16, 0.12)
DECAY = (0.0, 0.03)
REPULSION = 1.0
ADHESION = 0.35
REPEL_RANGE = 1.0
ADHERE_RANGE = 4.0
FORCE_SCALE = 0.08
CHEMOTAXIS = 1.5
SLOT_BLOCK = 512


def with_halo(block, sides, width):
    for axis, dim in sides:
        count = lax.axis_size(axis)
        forward = [(i, i + 1) for i in range(count - 1)]
        backward = [(target, source) for source, target in forward]
        low = lax.ppermute(
            lax.slice_in_dim(block, block.shape[dim] - width, None, axis=dim), axis, forward
        )
        high = lax.ppermute(lax.slice_in_dim(block, 0, width, axis=dim), axis, backward)
        block = jnp.concatenate([low, block, high], axis=dim)
    return block


def block_force(mine, others):
    offset = mine[:3, :, :, None, None] - others[:3, :, None, :, :]
    distance = jnp.sum(offset * offset, axis=0)
    strength = REPULSION * jnp.exp(-distance / REPEL_RANGE) - ADHESION * jnp.exp(
        -distance / ADHERE_RANGE
    )
    weight = mine[3][:, :, None, None] * others[3][:, None, :, :] * strength
    return jnp.sum(offset * weight[None], axis=(3, 4))


def relax(padded):
    center = padded[:, 1:-1, 1:-1]
    sideways = jnp.pad(center, ((0, 0), (0, 0), (0, 0), (1, 1)))
    beside_all = padded[:, 2:, 1:-1] + padded[:, :-2, 1:-1]
    beside_all = beside_all + padded[:, 1:-1, 2:] + padded[:, 1:-1, :-2]
    beside_all = beside_all + sideways[..., 2:] + sideways[..., :-2]
    spread = jnp.array(DIFFUSION, jnp.float32)[:, None, None, None]
    losses = jnp.array(DECAY, jnp.float32)[:, None, None, None]
    return center + spread * (beside_all - 6.0 * center) - losses * center


def routing(sends, length):
    ends = jnp.cumsum(sends)
    starts = ends - sends
    cell = jnp.arange(length, dtype=jnp.int32)
    target = jnp.sum((ends[:, None] <= cell[None, :]).astype(jnp.int32), axis=0)
    routed = target < sends.shape[0]
    target = jnp.minimum(target, sends.shape[0] - 1)
    lanes = jnp.arange(sends.shape[0], dtype=jnp.int32)
    first = jnp.sum(jnp.where(lanes[:, None] == target[None, :], starts[:, None], 0), axis=0)
    return (target, cell - first, routed)


def hot_tables(piece, planes, columns, kind=jnp.float32):
    row_hot = (piece[:, None] // columns == jnp.arange(planes, dtype=jnp.int32)[None, :]).astype(
        kind
    )
    column_hot = (piece[:, None] % columns == jnp.arange(columns, dtype=jnp.int32)[None, :]).astype(
        kind
    )
    return (row_hot, column_hot)


def split_three(values):
    high = lax.reduce_precision(values, exponent_bits=8, mantissa_bits=7)
    rest = values - high
    middle = lax.reduce_precision(rest, exponent_bits=8, mantissa_bits=7)
    return jnp.stack([high, middle, rest - middle]).astype(jnp.bfloat16)


def pick_exact(fields, reached, block):
    species, planes, columns = fields.shape
    parts = split_three(fields)
    pieces = reached.reshape(-1, block)

    def one_piece(piece):
        row_hot, column_hot = hot_tables(piece, planes, columns, jnp.bfloat16)
        picked = jnp.einsum(
            "psrx,mx->psrm", parts, column_hot, preferred_element_type=jnp.float32
        )
        picked = picked[0] + picked[1] + picked[2]
        return jnp.sum(picked * jnp.transpose(row_hot).astype(jnp.float32)[None], axis=1)

    found = lax.map(one_piece, pieces)
    return jnp.moveaxis(found, 1, 0).reshape(species, -1)


def pick_voxels(fields, reached):
    species, planes, columns = fields.shape
    pieces = reached.reshape(-1, SLOT_BLOCK)

    def one_piece(piece):
        row_hot, column_hot = hot_tables(piece, planes, columns)
        picked = jnp.einsum("srx,mx->srm", fields, column_hot, precision=lax.Precision.HIGHEST)
        return jnp.sum(picked * jnp.transpose(row_hot)[None], axis=1)

    found = lax.map(one_piece, pieces)
    return jnp.moveaxis(found, 1, 0).reshape(species, -1)


def spread_voxels(amounts, reached, planes, columns):
    species = amounts.shape[0]
    pieces = reached.reshape(-1, SLOT_BLOCK)
    shares = jnp.moveaxis(amounts.reshape(species, -1, SLOT_BLOCK), 1, 0)

    def add_piece(total, item):
        piece, share = item
        row_hot, column_hot = hot_tables(piece, planes, columns)
        weighted = share[:, :, None] * row_hot[None]
        return (
            total
            + jnp.einsum("smr,mx->srx", weighted, column_hot, precision=lax.Precision.HIGHEST),
            None,
        )

    empty = jnp.zeros((species, planes, columns), jnp.float32)
    total, unused = lax.scan(add_piece, empty, (pieces, shares))
    return total


def force_kernel(chosen_ref, rows_ref, cols_ref, out_ref):
    blocks = out_ref.shape[0]
    picks = chosen_ref.shape[0] // blocks
    chunks = cols_ref.shape[2] // 8
    shape = (8, cols_ref.shape[3])

    def one_block(block, carry):
        own = rows_ref[block + HB]
        mine = [jnp.broadcast_to(own[axis:axis + 1, :], shape) for axis in range(4)]

        def one_pick(pick, totals):
            other = chosen_ref[block * picks + pick]
            totals = list(totals)
            for chunk in range(chunks):
                part = pl.ds(chunk * 8, 8)
                offset = [mine[axis] - cols_ref[other, axis, part, :] for axis in range(3)]
                distance = offset[0] * offset[0] + offset[1] * offset[1] + offset[2] * offset[2]
                strength = REPULSION * jnp.exp(-distance / REPEL_RANGE) - ADHESION * jnp.exp(
                    -distance / ADHERE_RANGE
                )
                weight = mine[3] * cols_ref[other, 3, part, :] * strength
                for axis in range(3):
                    totals[axis] = totals[axis] + offset[axis] * weight
            return tuple(totals)

        zero = jnp.zeros(shape, jnp.float32)
        totals = lax.fori_loop(0, picks, one_pick, (zero, zero, zero))
        out_ref[block] = jnp.concatenate(
            [jnp.sum(total, axis=0, keepdims=True) for total in totals], axis=0
        )
        return carry

    lax.fori_loop(0, blocks, one_block, 0)


def pair_forces(extended, neighbor_blocks):
    coords, span, lanes = extended.shape
    blocks, picks = neighbor_blocks.shape
    rows = jnp.transpose(extended, (1, 0, 2))
    cols = jnp.broadcast_to(rows[:, :, :, None], (span, coords, lanes, lanes))
    pairs = blocks * picks * lanes * lanes
    out = pl.pallas_call(
        force_kernel,
        out_shape=jax.ShapeDtypeStruct((blocks, 3, lanes), jnp.float32),
        in_specs=[
            pl.BlockSpec(memory_space=pltpu.SMEM),
            pl.BlockSpec(memory_space=pltpu.VMEM),
            pl.BlockSpec(memory_space=pltpu.VMEM),
        ],
        out_specs=pl.BlockSpec(memory_space=pltpu.VMEM),
        cost_estimate=pl.CostEstimate(
            flops=26 * pairs, transcendentals=2 * pairs, bytes_accessed=4 * cols.size
        ),
    )(neighbor_blocks.reshape(-1), rows, cols)
    return jnp.transpose(out, (1, 0, 2))


def neighbours(block, axis, dim):
    count = lax.axis_size(axis)
    forward = [(i, i + 1) for i in range(count - 1)]
    backward = [(target, source) for source, target in forward]
    low = lax.ppermute(lax.slice_in_dim(block, block.shape[dim] - 1, None, axis=dim), axis, forward)
    high = lax.ppermute(lax.slice_in_dim(block, 0, 1, axis=dim), axis, backward)
    return (low, high)


def shifted(block, low, high, dim):
    size = block.shape[dim]
    up = jnp.concatenate([lax.slice_in_dim(block, 1, size, axis=dim), high], axis=dim)
    down = jnp.concatenate([low, lax.slice_in_dim(block, 0, size - 1, axis=dim)], axis=dim)
    return (up, down)


def relax_step(center):
    z_low, z_high = neighbours(center, "slab", 1)
    y_low, y_high = neighbours(center, "tile", 2)
    z_up, z_down = shifted(center, z_low, z_high, 1)
    y_up, y_down = shifted(center, y_low, y_high, 2)
    sideways = jnp.pad(center, ((0, 0), (0, 0), (0, 0), (1, 1)))
    beside_all = z_up + z_down
    beside_all = beside_all + y_up + y_down
    beside_all = beside_all + sideways[..., 2:] + sideways[..., :-2]
    spread = jnp.array(DIFFUSION, jnp.float32)[:, None, None, None]
    losses = jnp.array(DECAY, jnp.float32)[:, None, None, None]
    return center + spread * (beside_all - 6.0 * center) - losses * center


def bits_of(width):
    return max(1, (width - 1).bit_length())


def gather_windows(values, starts, length):
    channels, cells = values.shape
    width = cells + length
    rows = starts.shape[0]
    padded = jnp.pad(values, ((0, 0), (0, length)))
    held = jnp.broadcast_to(padded[:, None, :], (channels, rows, width))
    for bit in range(bits_of(cells)):
        step = 1 << bit
        take = ((starts >> bit) & 1 == 1)[None, :, None]
        held = jnp.where(take, jnp.roll(held, -step, axis=2), held)
    return held[:, :, :length]


def scatter_windows(windows, starts, cells):
    channels, rows, length = windows.shape
    width = cells + length
    held = jnp.pad(windows, ((0, 0), (0, 0), (0, width - length)))
    for bit in range(bits_of(cells)):
        step = 1 << bit
        take = ((starts >> bit) & 1 == 1)[None, :, None]
        held = jnp.where(take, jnp.roll(held, step, axis=2), held)
    return jnp.sum(held[:, :, :cells], axis=1)


def local(
    positions, radius, uptake_rate, voxel_local, cell_counts, send_counts, neighbor_blocks, field
):
    tiles = lax.axis_size("tile")
    capacity = positions.shape[1]
    blocks = capacity // 128
    slot_size = 2 * capacity // tiles
    cell = jnp.arange(capacity, dtype=jnp.int32)
    count = cell_counts[0]
    kept = jnp.where(cell < count, radius, 0.0)
    table = jnp.concatenate([positions, kept[None]], axis=0)
    extended = with_halo(table, (("tile", 1),), HB * 128)
    extended = extended.reshape(4, blocks + 2 * HB, 128)
    forces = pair_forces(extended, neighbor_blocks).reshape(3, capacity)
    sends = send_counts[0]
    ends = jnp.cumsum(sends)
    starts = ends - sends
    ranks = jnp.arange(slot_size, dtype=jnp.int32)
    valid = ranks[None, :] < sends[:, None]
    payload = jnp.stack([voxel_local.astype(jnp.float32), uptake_rate])
    windows = gather_windows(payload, starts, slot_size)
    windows = jnp.where(valid[None], windows, 0.0)
    arrived = lax.all_to_all(windows, "tile", split_axis=1, concat_axis=1, tiled=True)
    reached = arrived[0].reshape(-1).astype(jnp.int32)
    rates = arrived[1].reshape(-1)
    species, depth, rows, columns = field.shape
    planes = depth * rows
    oxygen_rows = field[0].reshape(1, planes, columns)
    oxygen = pick_exact(oxygen_rows, reached, 2 * SLOT_BLOCK)[0]
    consume = rates * oxygen / (MICHAELIS_HALF + oxygen)
    secrete = SECRETION * rates * HYPOXIA_HALF / (HYPOXIA_HALF + oxygen)
    amounts = jnp.stack([-STEP_TIME * consume, STEP_TIME * secrete])
    added = spread_voxels(amounts, reached, planes, columns)
    state = field + added.reshape(species, depth, rows, columns)
    for step in range(ITERS):
        state = relax_step(state)
    vegf = state[1]
    z_low, z_high = neighbours(vegf, "slab", 0)
    y_low, y_high = neighbours(vegf, "tile", 1)
    z_up, z_down = shifted(vegf, z_low, z_high, 0)
    y_up, y_down = shifted(vegf, y_low, y_high, 1)
    rise_z = 0.5 * (z_up - z_down)
    rise_y = 0.5 * (y_up - y_down)
    middle = jnp.pad(vegf, ((0, 0), (0, 0), (1, 1)))
    rise_x = 0.5 * (middle[..., 2:] - middle[..., :-2])
    rises = jnp.stack([rise_z, rise_y, rise_x]).reshape(3, planes, columns)
    slopes = pick_voxels(rises, reached).reshape(3, tiles, slot_size)
    returned = lax.all_to_all(slopes, "tile", split_axis=1, concat_axis=1, tiled=True)
    returned = jnp.where(valid[None], returned, 0.0)
    slope = scatter_windows(returned, starts, capacity)
    velocity = FORCE_SCALE * forces + CHEMOTAXIS * slope
    return (velocity, state)


def solution(mesh):
    placed = (
        P(None, ("slab", "tile")),
        P(("slab", "tile")),
        P(("slab", "tile")),
        P(("slab", "tile")),
        P(("slab", "tile")),
        P(("slab", "tile"), None),
        P(("slab", "tile"), None),
        P(None, "slab", "tile", None),
    )
    return jax.shard_map(
        local,
        mesh=mesh,
        in_specs=placed,
        out_specs=(P(None, ("slab", "tile")), P(None, "slab", "tile", None)),
        check_vma=False,
    )
```

```python
import jax
import jax.numpy as jnp
from jax import lax
from jax.experimental import pallas as pl
from jax.experimental.pallas import tpu as pltpu
from jax.sharding import PartitionSpec as P

HB = 4
K = 8
ITERS = 4


MICHAELIS_HALF = 0.5
HYPOXIA_HALF = 0.6
SECRETION = 0.4
STEP_TIME = 0.5
DIFFUSION = (0.16, 0.12)
DECAY = (0.0, 0.03)
REPULSION = 1.0
ADHESION = 0.35
REPEL_RANGE = 1.0
ADHERE_RANGE = 4.0
FORCE_SCALE = 0.08
CHEMOTAXIS = 1.5
SLOT_BLOCK = 512


def with_halo(block, sides, width):
    for axis, dim in sides:
        count = lax.axis_size(axis)
        forward = [(i, i + 1) for i in range(count - 1)]
        backward = [(target, source) for source, target in forward]
        low = lax.ppermute(
            lax.slice_in_dim(block, block.shape[dim] - width, None, axis=dim), axis, forward
        )
        high = lax.ppermute(lax.slice_in_dim(block, 0, width, axis=dim), axis, backward)
        block = jnp.concatenate([low, block, high], axis=dim)
    return block


def block_force(mine, others):
    offset = mine[:3, :, :, None, None] - others[:3, :, None, :, :]
    distance = jnp.sum(offset * offset, axis=0)
    strength = REPULSION * jnp.exp(-distance / REPEL_RANGE) - ADHESION * jnp.exp(
        -distance / ADHERE_RANGE
    )
    weight = mine[3][:, :, None, None] * others[3][:, None, :, :] * strength
    return jnp.sum(offset * weight[None], axis=(3, 4))


def relax(padded):
    center = padded[:, 1:-1, 1:-1]
    sideways = jnp.pad(center, ((0, 0), (0, 0), (0, 0), (1, 1)))
    beside_all = padded[:, 2:, 1:-1] + padded[:, :-2, 1:-1]
    beside_all = beside_all + padded[:, 1:-1, 2:] + padded[:, 1:-1, :-2]
    beside_all = beside_all + sideways[..., 2:] + sideways[..., :-2]
    spread = jnp.array(DIFFUSION, jnp.float32)[:, None, None, None]
    losses = jnp.array(DECAY, jnp.float32)[:, None, None, None]
    return center + spread * (beside_all - 6.0 * center) - losses * center


def routing(sends, length):
    ends = jnp.cumsum(sends)
    starts = ends - sends
    cell = jnp.arange(length, dtype=jnp.int32)
    target = jnp.sum((ends[:, None] <= cell[None, :]).astype(jnp.int32), axis=0)
    routed = target < sends.shape[0]
    target = jnp.minimum(target, sends.shape[0] - 1)
    lanes = jnp.arange(sends.shape[0], dtype=jnp.int32)
    first = jnp.sum(jnp.where(lanes[:, None] == target[None, :], starts[:, None], 0), axis=0)
    return (target, cell - first, routed)


def hot_tables(piece, planes, columns, kind=jnp.float32):
    row_hot = (piece[:, None] // columns == jnp.arange(planes, dtype=jnp.int32)[None, :]).astype(
        kind
    )
    column_hot = (piece[:, None] % columns == jnp.arange(columns, dtype=jnp.int32)[None, :]).astype(
        kind
    )
    return (row_hot, column_hot)


def split_three(values):
    high = lax.reduce_precision(values, exponent_bits=8, mantissa_bits=7)
    rest = values - high
    middle = lax.reduce_precision(rest, exponent_bits=8, mantissa_bits=7)
    return jnp.stack([high, middle, rest - middle]).astype(jnp.bfloat16)


def pick_exact(fields, reached, block):
    species, planes, columns = fields.shape
    parts = split_three(fields)
    pieces = reached.reshape(-1, block)

    def one_piece(piece):
        row_hot, column_hot = hot_tables(piece, planes, columns, jnp.bfloat16)
        picked = jnp.einsum(
            "psrx,mx->psrm", parts, column_hot, preferred_element_type=jnp.float32
        )
        picked = picked[0] + picked[1] + picked[2]
        return jnp.sum(picked * jnp.transpose(row_hot).astype(jnp.float32)[None], axis=1)

    found = lax.map(one_piece, pieces)
    return jnp.moveaxis(found, 1, 0).reshape(species, -1)


def pick_voxels(fields, reached):
    species, planes, columns = fields.shape
    pieces = reached.reshape(-1, SLOT_BLOCK)

    def one_piece(piece):
        row_hot, column_hot = hot_tables(piece, planes, columns)
        picked = jnp.einsum("srx,mx->srm", fields, column_hot, precision=lax.Precision.HIGHEST)
        return jnp.sum(picked * jnp.transpose(row_hot)[None], axis=1)

    found = lax.map(one_piece, pieces)
    return jnp.moveaxis(found, 1, 0).reshape(species, -1)


def spread_voxels(amounts, reached, planes, columns):
    species = amounts.shape[0]
    pieces = reached.reshape(-1, SLOT_BLOCK)
    shares = jnp.moveaxis(amounts.reshape(species, -1, SLOT_BLOCK), 1, 0)

    def add_piece(total, item):
        piece, share = item
        row_hot, column_hot = hot_tables(piece, planes, columns)
        weighted = share[:, :, None] * row_hot[None]
        return (
            total
            + jnp.einsum("smr,mx->srx", weighted, column_hot, precision=lax.Precision.HIGHEST),
            None,
        )

    empty = jnp.zeros((species, planes, columns), jnp.float32)
    total, unused = lax.scan(add_piece, empty, (pieces, shares))
    return total


def force_kernel(chosen_ref, rows_ref, cols_ref, out_ref):
    blocks = out_ref.shape[0]
    picks = chosen_ref.shape[0] // blocks
    chunks = cols_ref.shape[2] // 8
    shape = (8, rows_ref.shape[2])

    def one_block(block, carry):
        own = rows_ref[block + HB]
        mine = [jnp.broadcast_to(own[axis:axis + 1, :], shape) for axis in range(4)]

        def one_pick(pick, totals):
            other = chosen_ref[block * picks + pick]
            totals = list(totals)
            for chunk in range(chunks):
                part = pl.ds(chunk * 8, 8)
                offset = [mine[axis] - jnp.broadcast_to(cols_ref[other, axis, part, :], shape) for axis in range(3)]
                distance = offset[0] * offset[0] + offset[1] * offset[1] + offset[2] * offset[2]
                strength = REPULSION * jnp.exp(-distance / REPEL_RANGE) - ADHESION * jnp.exp(
                    -distance / ADHERE_RANGE
                )
                weight = mine[3] * jnp.broadcast_to(cols_ref[other, 3, part, :], shape) * strength
                for axis in range(3):
                    totals[axis] = totals[axis] + offset[axis] * weight
            return tuple(totals)

        zero = jnp.zeros(shape, jnp.float32)
        totals = lax.fori_loop(0, picks, one_pick, (zero, zero, zero))
        out_ref[block] = jnp.concatenate(
            [jnp.sum(total, axis=0, keepdims=True) for total in totals], axis=0
        )
        return carry

    lax.fori_loop(0, blocks, one_block, 0)


def pair_forces(extended, neighbor_blocks):
    coords, span, lanes = extended.shape
    blocks, picks = neighbor_blocks.shape
    rows = jnp.transpose(extended, (1, 0, 2))
    cols = rows[:, :, :, None]
    pairs = blocks * picks * lanes * lanes
    out = pl.pallas_call(
        force_kernel,
        out_shape=jax.ShapeDtypeStruct((blocks, 3, lanes), jnp.float32),
        in_specs=[
            pl.BlockSpec(memory_space=pltpu.SMEM),
            pl.BlockSpec(memory_space=pltpu.VMEM),
            pl.BlockSpec(memory_space=pltpu.VMEM),
        ],
        out_specs=pl.BlockSpec(memory_space=pltpu.VMEM),
        cost_estimate=pl.CostEstimate(
            flops=26 * pairs, transcendentals=2 * pairs, bytes_accessed=4 * cols.size
        ),
    )(neighbor_blocks.reshape(-1), rows, cols)
    return jnp.transpose(out, (1, 0, 2))


def neighbours(block, axis, dim):
    count = lax.axis_size(axis)
    forward = [(i, i + 1) for i in range(count - 1)]
    backward = [(target, source) for source, target in forward]
    low = lax.ppermute(lax.slice_in_dim(block, block.shape[dim] - 1, None, axis=dim), axis, forward)
    high = lax.ppermute(lax.slice_in_dim(block, 0, 1, axis=dim), axis, backward)
    return (low, high)


def shifted(block, low, high, dim):
    size = block.shape[dim]
    up = jnp.concatenate([lax.slice_in_dim(block, 1, size, axis=dim), high], axis=dim)
    down = jnp.concatenate([low, lax.slice_in_dim(block, 0, size - 1, axis=dim)], axis=dim)
    return (up, down)


def relax_step(center):
    z_low, z_high = neighbours(center, "slab", 1)
    y_low, y_high = neighbours(center, "tile", 2)
    z_up, z_down = shifted(center, z_low, z_high, 1)
    y_up, y_down = shifted(center, y_low, y_high, 2)
    sideways = jnp.pad(center, ((0, 0), (0, 0), (0, 0), (1, 1)))
    beside_all = z_up + z_down
    beside_all = beside_all + y_up + y_down
    beside_all = beside_all + sideways[..., 2:] + sideways[..., :-2]
    spread = jnp.array(DIFFUSION, jnp.float32)[:, None, None, None]
    losses = jnp.array(DECAY, jnp.float32)[:, None, None, None]
    return center + spread * (beside_all - 6.0 * center) - losses * center


def bits_of(width):
    return max(1, (width - 1).bit_length())


def gather_windows(values, starts, length):
    channels, cells = values.shape
    width = cells + length
    rows = starts.shape[0]
    padded = jnp.pad(values, ((0, 0), (0, length)))
    held = jnp.broadcast_to(padded[:, None, :], (channels, rows, width))
    for bit in range(bits_of(cells)):
        step = 1 << bit
        take = ((starts >> bit) & 1 == 1)[None, :, None]
        held = jnp.where(take, jnp.roll(held, -step, axis=2), held)
    return held[:, :, :length]


def scatter_windows(windows, starts, cells):
    channels, rows, length = windows.shape
    width = cells + length
    held = jnp.pad(windows, ((0, 0), (0, 0), (0, width - length)))
    for bit in range(bits_of(cells)):
        step = 1 << bit
        take = ((starts >> bit) & 1 == 1)[None, :, None]
        held = jnp.where(take, jnp.roll(held, step, axis=2), held)
    return jnp.sum(held[:, :, :cells], axis=1)


def local(
    positions, radius, uptake_rate, voxel_local, cell_counts, send_counts, neighbor_blocks, field
):
    tiles = lax.axis_size("tile")
    capacity = positions.shape[1]
    blocks = capacity // 128
    slot_size = 2 * capacity // tiles
    cell = jnp.arange(capacity, dtype=jnp.int32)
    count = cell_counts[0]
    kept = jnp.where(cell < count, radius, 0.0)
    table = jnp.concatenate([positions, kept[None]], axis=0)
    extended = with_halo(table, (("tile", 1),), HB * 128)
    extended = extended.reshape(4, blocks + 2 * HB, 128)
    forces = pair_forces(extended, neighbor_blocks).reshape(3, capacity)
    sends = send_counts[0]
    ends = jnp.cumsum(sends)
    starts = ends - sends
    ranks = jnp.arange(slot_size, dtype=jnp.int32)
    valid = ranks[None, :] < sends[:, None]
    payload = jnp.stack([voxel_local.astype(jnp.float32), uptake_rate])
    windows = gather_windows(payload, starts, slot_size)
    windows = jnp.where(valid[None], windows, 0.0)
    arrived = lax.all_to_all(windows, "tile", split_axis=1, concat_axis=1, tiled=True)
    reached = arrived[0].reshape(-1).astype(jnp.int32)
    rates = arrived[1].reshape(-1)
    species, depth, rows, columns = field.shape
    planes = depth * rows
    oxygen_rows = field[0].reshape(1, planes, columns)
    oxygen = pick_exact(oxygen_rows, reached, 2 * SLOT_BLOCK)[0]
    consume = rates * oxygen / (MICHAELIS_HALF + oxygen)
    secrete = SECRETION * rates * HYPOXIA_HALF / (HYPOXIA_HALF + oxygen)
    amounts = jnp.stack([-STEP_TIME * consume, STEP_TIME * secrete])
    added = spread_voxels(amounts, reached, planes, columns)
    state = field + added.reshape(species, depth, rows, columns)
    for step in range(ITERS):
        state = relax_step(state)
    vegf = state[1]
    z_low, z_high = neighbours(vegf, "slab", 0)
    y_low, y_high = neighbours(vegf, "tile", 1)
    z_up, z_down = shifted(vegf, z_low, z_high, 0)
    y_up, y_down = shifted(vegf, y_low, y_high, 1)
    rise_z = 0.5 * (z_up - z_down)
    rise_y = 0.5 * (y_up - y_down)
    middle = jnp.pad(vegf, ((0, 0), (0, 0), (1, 1)))
    rise_x = 0.5 * (middle[..., 2:] - middle[..., :-2])
    rises = jnp.stack([rise_z, rise_y, rise_x]).reshape(3, planes, columns)
    slopes = pick_voxels(rises, reached).reshape(3, tiles, slot_size)
    returned = lax.all_to_all(slopes, "tile", split_axis=1, concat_axis=1, tiled=True)
    returned = jnp.where(valid[None], returned, 0.0)
    slope = scatter_windows(returned, starts, capacity)
    velocity = FORCE_SCALE * forces + CHEMOTAXIS * slope
    return (velocity, state)


def solution(mesh):
    placed = (
        P(None, ("slab", "tile")),
        P(("slab", "tile")),
        P(("slab", "tile")),
        P(("slab", "tile")),
        P(("slab", "tile")),
        P(("slab", "tile"), None),
        P(("slab", "tile"), None),
        P(None, "slab", "tile", None),
    )
    return jax.shard_map(
        local,
        mesh=mesh,
        in_specs=placed,
        out_specs=(P(None, ("slab", "tile")), P(None, "slab", "tile", None)),
        check_vma=False,
    )
```

```python
import jax
import jax.numpy as jnp
from jax import lax
from jax.experimental import pallas as pl
from jax.experimental.pallas import tpu as pltpu
from jax.sharding import PartitionSpec as P

HB = 4
K = 8
ITERS = 4


MICHAELIS_HALF = 0.5
HYPOXIA_HALF = 0.6
SECRETION = 0.4
STEP_TIME = 0.5
DIFFUSION = (0.16, 0.12)
DECAY = (0.0, 0.03)
REPULSION = 1.0
ADHESION = 0.35
REPEL_RANGE = 1.0
ADHERE_RANGE = 4.0
FORCE_SCALE = 0.08
CHEMOTAXIS = 1.5
SLOT_BLOCK = 256


def with_halo(block, sides, width):
    for axis, dim in sides:
        count = lax.axis_size(axis)
        forward = [(i, i + 1) for i in range(count - 1)]
        backward = [(target, source) for source, target in forward]
        low = lax.ppermute(
            lax.slice_in_dim(block, block.shape[dim] - width, None, axis=dim), axis, forward
        )
        high = lax.ppermute(lax.slice_in_dim(block, 0, width, axis=dim), axis, backward)
        block = jnp.concatenate([low, block, high], axis=dim)
    return block


def block_force(mine, others):
    offset = mine[:3, :, :, None, None] - others[:3, :, None, :, :]
    distance = jnp.sum(offset * offset, axis=0)
    strength = REPULSION * jnp.exp(-distance / REPEL_RANGE) - ADHESION * jnp.exp(
        -distance / ADHERE_RANGE
    )
    weight = mine[3][:, :, None, None] * others[3][:, None, :, :] * strength
    return jnp.sum(offset * weight[None], axis=(3, 4))


def relax(padded):
    center = padded[:, 1:-1, 1:-1]
    sideways = jnp.pad(center, ((0, 0), (0, 0), (0, 0), (1, 1)))
    beside_all = padded[:, 2:, 1:-1] + padded[:, :-2, 1:-1]
    beside_all = beside_all + padded[:, 1:-1, 2:] + padded[:, 1:-1, :-2]
    beside_all = beside_all + sideways[..., 2:] + sideways[..., :-2]
    spread = jnp.array(DIFFUSION, jnp.float32)[:, None, None, None]
    losses = jnp.array(DECAY, jnp.float32)[:, None, None, None]
    return center + spread * (beside_all - 6.0 * center) - losses * center


def routing(sends, length):
    ends = jnp.cumsum(sends)
    starts = ends - sends
    cell = jnp.arange(length, dtype=jnp.int32)
    target = jnp.sum((ends[:, None] <= cell[None, :]).astype(jnp.int32), axis=0)
    routed = target < sends.shape[0]
    target = jnp.minimum(target, sends.shape[0] - 1)
    lanes = jnp.arange(sends.shape[0], dtype=jnp.int32)
    first = jnp.sum(jnp.where(lanes[:, None] == target[None, :], starts[:, None], 0), axis=0)
    return (target, cell - first, routed)


def hot_tables(piece, planes, columns, kind=jnp.float32):
    row_hot = (piece[:, None] // columns == jnp.arange(planes, dtype=jnp.int32)[None, :]).astype(
        kind
    )
    column_hot = (piece[:, None] % columns == jnp.arange(columns, dtype=jnp.int32)[None, :]).astype(
        kind
    )
    return (row_hot, column_hot)


def split_three(values):
    high = lax.reduce_precision(values, exponent_bits=8, mantissa_bits=7)
    rest = values - high
    middle = lax.reduce_precision(rest, exponent_bits=8, mantissa_bits=7)
    return jnp.stack([high, middle, rest - middle]).astype(jnp.bfloat16)


def pick_exact(fields, reached, block):
    species, planes, columns = fields.shape
    parts = split_three(fields)
    pieces = reached.reshape(-1, block)

    def one_piece(piece):
        row_hot, column_hot = hot_tables(piece, planes, columns, jnp.bfloat16)
        picked = jnp.einsum(
            "psrx,mx->psrm", parts, column_hot, preferred_element_type=jnp.float32
        )
        picked = picked[0] + picked[1] + picked[2]
        return jnp.sum(picked * jnp.transpose(row_hot).astype(jnp.float32)[None], axis=1)

    found = lax.map(one_piece, pieces)
    return jnp.moveaxis(found, 1, 0).reshape(species, -1)


def pick_voxels(fields, reached):
    species, planes, columns = fields.shape
    pieces = reached.reshape(-1, SLOT_BLOCK)

    def one_piece(piece):
        row_hot, column_hot = hot_tables(piece, planes, columns)
        picked = jnp.einsum("srx,mx->srm", fields, column_hot, precision=lax.Precision.HIGHEST)
        return jnp.sum(picked * jnp.transpose(row_hot)[None], axis=1)

    found = lax.map(one_piece, pieces)
    return jnp.moveaxis(found, 1, 0).reshape(species, -1)


def spread_voxels(amounts, reached, planes, columns):
    species = amounts.shape[0]
    pieces = reached.reshape(-1, SLOT_BLOCK)
    shares = jnp.moveaxis(amounts.reshape(species, -1, SLOT_BLOCK), 1, 0)

    def add_piece(total, item):
        piece, share = item
        row_hot, column_hot = hot_tables(piece, planes, columns)
        weighted = share[:, :, None] * row_hot[None]
        return (
            total
            + jnp.einsum("smr,mx->srx", weighted, column_hot, precision=lax.Precision.HIGHEST),
            None,
        )

    empty = jnp.zeros((species, planes, columns), jnp.float32)
    total, unused = lax.scan(add_piece, empty, (pieces, shares))
    return total


def force_kernel(chosen_ref, rows_ref, cols_ref, out_ref):
    blocks = out_ref.shape[0]
    picks = chosen_ref.shape[0] // blocks
    chunks = cols_ref.shape[2] // 8
    shape = (8, cols_ref.shape[3])

    def one_block(block, carry):
        own = rows_ref[block + HB]
        mine = [jnp.broadcast_to(own[axis:axis + 1, :], shape) for axis in range(4)]

        def one_pick(pick, totals):
            other = chosen_ref[block * picks + pick]
            totals = list(totals)
            for chunk in range(chunks):
                part = pl.ds(chunk * 8, 8)
                offset = [mine[axis] - cols_ref[other, axis, part, :] for axis in range(3)]
                distance = offset[0] * offset[0] + offset[1] * offset[1] + offset[2] * offset[2]
                strength = REPULSION * jnp.exp(-distance / REPEL_RANGE) - ADHESION * jnp.exp(
                    -distance / ADHERE_RANGE
                )
                weight = mine[3] * cols_ref[other, 3, part, :] * strength
                for axis in range(3):
                    totals[axis] = totals[axis] + offset[axis] * weight
            return tuple(totals)

        zero = jnp.zeros(shape, jnp.float32)
        totals = lax.fori_loop(0, picks, one_pick, (zero, zero, zero))
        out_ref[block] = jnp.concatenate(
            [jnp.sum(total, axis=0, keepdims=True) for total in totals], axis=0
        )
        return carry

    lax.fori_loop(0, blocks, one_block, 0)


def pair_forces(extended, neighbor_blocks):
    coords, span, lanes = extended.shape
    blocks, picks = neighbor_blocks.shape
    rows = jnp.transpose(extended, (1, 0, 2))
    cols = jnp.broadcast_to(rows[:, :, :, None], (span, coords, lanes, lanes))
    pairs = blocks * picks * lanes * lanes
    out = pl.pallas_call(
        force_kernel,
        out_shape=jax.ShapeDtypeStruct((blocks, 3, lanes), jnp.float32),
        in_specs=[
            pl.BlockSpec(memory_space=pltpu.SMEM),
            pl.BlockSpec(memory_space=pltpu.VMEM),
            pl.BlockSpec(memory_space=pltpu.VMEM),
        ],
        out_specs=pl.BlockSpec(memory_space=pltpu.VMEM),
        cost_estimate=pl.CostEstimate(
            flops=26 * pairs, transcendentals=2 * pairs, bytes_accessed=4 * cols.size
        ),
    )(neighbor_blocks.reshape(-1), rows, cols)
    return jnp.transpose(out, (1, 0, 2))


def neighbours(block, axis, dim):
    count = lax.axis_size(axis)
    forward = [(i, i + 1) for i in range(count - 1)]
    backward = [(target, source) for source, target in forward]
    low = lax.ppermute(lax.slice_in_dim(block, block.shape[dim] - 1, None, axis=dim), axis, forward)
    high = lax.ppermute(lax.slice_in_dim(block, 0, 1, axis=dim), axis, backward)
    return (low, high)


def shifted(block, low, high, dim):
    size = block.shape[dim]
    up = jnp.concatenate([lax.slice_in_dim(block, 1, size, axis=dim), high], axis=dim)
    down = jnp.concatenate([low, lax.slice_in_dim(block, 0, size - 1, axis=dim)], axis=dim)
    return (up, down)


def relax_step(center):
    z_low, z_high = neighbours(center, "slab", 1)
    y_low, y_high = neighbours(center, "tile", 2)
    z_up, z_down = shifted(center, z_low, z_high, 1)
    y_up, y_down = shifted(center, y_low, y_high, 2)
    sideways = jnp.pad(center, ((0, 0), (0, 0), (0, 0), (1, 1)))
    beside_all = z_up + z_down
    beside_all = beside_all + y_up + y_down
    beside_all = beside_all + sideways[..., 2:] + sideways[..., :-2]
    spread = jnp.array(DIFFUSION, jnp.float32)[:, None, None, None]
    losses = jnp.array(DECAY, jnp.float32)[:, None, None, None]
    return center + spread * (beside_all - 6.0 * center) - losses * center


def bits_of(width):
    return max(1, (width - 1).bit_length())


def gather_windows(values, starts, length):
    channels, cells = values.shape
    width = cells + length
    rows = starts.shape[0]
    padded = jnp.pad(values, ((0, 0), (0, length)))
    held = jnp.broadcast_to(padded[:, None, :], (channels, rows, width))
    for bit in range(bits_of(cells)):
        step = 1 << bit
        take = ((starts >> bit) & 1 == 1)[None, :, None]
        held = jnp.where(take, jnp.roll(held, -step, axis=2), held)
    return held[:, :, :length]


def scatter_windows(windows, starts, cells):
    channels, rows, length = windows.shape
    width = cells + length
    held = jnp.pad(windows, ((0, 0), (0, 0), (0, width - length)))
    for bit in range(bits_of(cells)):
        step = 1 << bit
        take = ((starts >> bit) & 1 == 1)[None, :, None]
        held = jnp.where(take, jnp.roll(held, step, axis=2), held)
    return jnp.sum(held[:, :, :cells], axis=1)


def local(
    positions, radius, uptake_rate, voxel_local, cell_counts, send_counts, neighbor_blocks, field
):
    tiles = lax.axis_size("tile")
    capacity = positions.shape[1]
    blocks = capacity // 128
    slot_size = 2 * capacity // tiles
    cell = jnp.arange(capacity, dtype=jnp.int32)
    count = cell_counts[0]
    kept = jnp.where(cell < count, radius, 0.0)
    table = jnp.concatenate([positions, kept[None]], axis=0)
    extended = with_halo(table, (("tile", 1),), HB * 128)
    extended = extended.reshape(4, blocks + 2 * HB, 128)
    forces = pair_forces(extended, neighbor_blocks).reshape(3, capacity)
    sends = send_counts[0]
    ends = jnp.cumsum(sends)
    starts = ends - sends
    ranks = jnp.arange(slot_size, dtype=jnp.int32)
    valid = ranks[None, :] < sends[:, None]
    payload = jnp.stack([voxel_local.astype(jnp.float32), uptake_rate])
    windows = gather_windows(payload, starts, slot_size)
    windows = jnp.where(valid[None], windows, 0.0)
    arrived = lax.all_to_all(windows, "tile", split_axis=1, concat_axis=1, tiled=True)
    reached = arrived[0].reshape(-1).astype(jnp.int32)
    rates = arrived[1].reshape(-1)
    species, depth, rows, columns = field.shape
    planes = depth * rows
    oxygen_rows = field[0].reshape(1, planes, columns)
    oxygen = pick_exact(oxygen_rows, reached, 4 * SLOT_BLOCK)[0]
    consume = rates * oxygen / (MICHAELIS_HALF + oxygen)
    secrete = SECRETION * rates * HYPOXIA_HALF / (HYPOXIA_HALF + oxygen)
    amounts = jnp.stack([-STEP_TIME * consume, STEP_TIME * secrete])
    added = spread_voxels(amounts, reached, planes, columns)
    state = field + added.reshape(species, depth, rows, columns)
    for step in range(ITERS):
        state = relax_step(state)
    vegf = state[1]
    z_low, z_high = neighbours(vegf, "slab", 0)
    y_low, y_high = neighbours(vegf, "tile", 1)
    z_up, z_down = shifted(vegf, z_low, z_high, 0)
    y_up, y_down = shifted(vegf, y_low, y_high, 1)
    rise_z = 0.5 * (z_up - z_down)
    rise_y = 0.5 * (y_up - y_down)
    middle = jnp.pad(vegf, ((0, 0), (0, 0), (1, 1)))
    rise_x = 0.5 * (middle[..., 2:] - middle[..., :-2])
    rises = jnp.stack([rise_z, rise_y, rise_x]).reshape(3, planes, columns)
    slopes = pick_voxels(rises, reached).reshape(3, tiles, slot_size)
    returned = lax.all_to_all(slopes, "tile", split_axis=1, concat_axis=1, tiled=True)
    returned = jnp.where(valid[None], returned, 0.0)
    slope = scatter_windows(returned, starts, capacity)
    velocity = FORCE_SCALE * forces + CHEMOTAXIS * slope
    return (velocity, state)


def solution(mesh):
    placed = (
        P(None, ("slab", "tile")),
        P(("slab", "tile")),
        P(("slab", "tile")),
        P(("slab", "tile")),
        P(("slab", "tile")),
        P(("slab", "tile"), None),
        P(("slab", "tile"), None),
        P(None, "slab", "tile", None),
    )
    return jax.shard_map(
        local,
        mesh=mesh,
        in_specs=placed,
        out_specs=(P(None, ("slab", "tile")), P(None, "slab", "tile", None)),
        check_vma=False,
    )
```

```python
import jax
import jax.numpy as jnp
from jax import lax
from jax.experimental import pallas as pl
from jax.experimental.pallas import tpu as pltpu
from jax.sharding import PartitionSpec as P

HB = 4
K = 8
ITERS = 4


MICHAELIS_HALF = 0.5
HYPOXIA_HALF = 0.6
SECRETION = 0.4
STEP_TIME = 0.5
DIFFUSION = (0.16, 0.12)
DECAY = (0.0, 0.03)
REPULSION = 1.0
ADHESION = 0.35
REPEL_RANGE = 1.0
ADHERE_RANGE = 4.0
FORCE_SCALE = 0.08
CHEMOTAXIS = 1.5
SLOT_BLOCK = 512
RADIX_BITS = 2


def with_halo(block, sides, width):
    for axis, dim in sides:
        count = lax.axis_size(axis)
        forward = [(i, i + 1) for i in range(count - 1)]
        backward = [(target, source) for source, target in forward]
        low = lax.ppermute(
            lax.slice_in_dim(block, block.shape[dim] - width, None, axis=dim), axis, forward
        )
        high = lax.ppermute(lax.slice_in_dim(block, 0, width, axis=dim), axis, backward)
        block = jnp.concatenate([low, block, high], axis=dim)
    return block


def block_force(mine, others):
    offset = mine[:3, :, :, None, None] - others[:3, :, None, :, :]
    distance = jnp.sum(offset * offset, axis=0)
    strength = REPULSION * jnp.exp(-distance / REPEL_RANGE) - ADHESION * jnp.exp(
        -distance / ADHERE_RANGE
    )
    weight = mine[3][:, :, None, None] * others[3][:, None, :, :] * strength
    return jnp.sum(offset * weight[None], axis=(3, 4))


def relax(padded):
    center = padded[:, 1:-1, 1:-1]
    sideways = jnp.pad(center, ((0, 0), (0, 0), (0, 0), (1, 1)))
    beside_all = padded[:, 2:, 1:-1] + padded[:, :-2, 1:-1]
    beside_all = beside_all + padded[:, 1:-1, 2:] + padded[:, 1:-1, :-2]
    beside_all = beside_all + sideways[..., 2:] + sideways[..., :-2]
    spread = jnp.array(DIFFUSION, jnp.float32)[:, None, None, None]
    losses = jnp.array(DECAY, jnp.float32)[:, None, None, None]
    return center + spread * (beside_all - 6.0 * center) - losses * center


def routing(sends, length):
    ends = jnp.cumsum(sends)
    starts = ends - sends
    cell = jnp.arange(length, dtype=jnp.int32)
    target = jnp.sum((ends[:, None] <= cell[None, :]).astype(jnp.int32), axis=0)
    routed = target < sends.shape[0]
    target = jnp.minimum(target, sends.shape[0] - 1)
    lanes = jnp.arange(sends.shape[0], dtype=jnp.int32)
    first = jnp.sum(jnp.where(lanes[:, None] == target[None, :], starts[:, None], 0), axis=0)
    return (target, cell - first, routed)


def hot_tables(piece, planes, columns, kind=jnp.float32):
    row_hot = (piece[:, None] // columns == jnp.arange(planes, dtype=jnp.int32)[None, :]).astype(
        kind
    )
    column_hot = (piece[:, None] % columns == jnp.arange(columns, dtype=jnp.int32)[None, :]).astype(
        kind
    )
    return (row_hot, column_hot)


def split_three(values):
    high = lax.reduce_precision(values, exponent_bits=8, mantissa_bits=7)
    rest = values - high
    middle = lax.reduce_precision(rest, exponent_bits=8, mantissa_bits=7)
    return jnp.stack([high, middle, rest - middle]).astype(jnp.bfloat16)


def pick_exact(fields, reached, block):
    species, planes, columns = fields.shape
    parts = split_three(fields)
    pieces = reached.reshape(-1, block)

    def one_piece(piece):
        row_hot, column_hot = hot_tables(piece, planes, columns, jnp.bfloat16)
        picked = jnp.einsum(
            "psrx,mx->psrm", parts, column_hot, preferred_element_type=jnp.float32
        )
        picked = picked[0] + picked[1] + picked[2]
        return jnp.sum(picked * jnp.transpose(row_hot).astype(jnp.float32)[None], axis=1)

    found = lax.map(one_piece, pieces)
    return jnp.moveaxis(found, 1, 0).reshape(species, -1)


def pick_voxels(fields, reached):
    species, planes, columns = fields.shape
    pieces = reached.reshape(-1, SLOT_BLOCK)

    def one_piece(piece):
        row_hot, column_hot = hot_tables(piece, planes, columns)
        picked = jnp.einsum("srx,mx->srm", fields, column_hot, precision=lax.Precision.HIGHEST)
        return jnp.sum(picked * jnp.transpose(row_hot)[None], axis=1)

    found = lax.map(one_piece, pieces)
    return jnp.moveaxis(found, 1, 0).reshape(species, -1)


def spread_voxels(amounts, reached, planes, columns):
    species = amounts.shape[0]
    pieces = reached.reshape(-1, SLOT_BLOCK)
    shares = jnp.moveaxis(amounts.reshape(species, -1, SLOT_BLOCK), 1, 0)

    def add_piece(total, item):
        piece, share = item
        row_hot, column_hot = hot_tables(piece, planes, columns)
        weighted = share[:, :, None] * row_hot[None]
        return (
            total
            + jnp.einsum("smr,mx->srx", weighted, column_hot, precision=lax.Precision.HIGHEST),
            None,
        )

    empty = jnp.zeros((species, planes, columns), jnp.float32)
    total, unused = lax.scan(add_piece, empty, (pieces, shares))
    return total


def force_kernel(chosen_ref, rows_ref, cols_ref, out_ref):
    blocks = out_ref.shape[0]
    picks = chosen_ref.shape[0] // blocks
    chunks = cols_ref.shape[2] // 8
    shape = (8, cols_ref.shape[3])

    def one_block(block, carry):
        own = rows_ref[block + HB]
        mine = [jnp.broadcast_to(own[axis:axis + 1, :], shape) for axis in range(4)]

        def one_pick(pick, totals):
            other = chosen_ref[block * picks + pick]
            totals = list(totals)
            for chunk in range(chunks):
                part = pl.ds(chunk * 8, 8)
                offset = [mine[axis] - cols_ref[other, axis, part, :] for axis in range(3)]
                distance = offset[0] * offset[0] + offset[1] * offset[1] + offset[2] * offset[2]
                strength = REPULSION * jnp.exp(-distance / REPEL_RANGE) - ADHESION * jnp.exp(
                    -distance / ADHERE_RANGE
                )
                weight = mine[3] * cols_ref[other, 3, part, :] * strength
                for axis in range(3):
                    totals[axis] = totals[axis] + offset[axis] * weight
            return tuple(totals)

        zero = jnp.zeros(shape, jnp.float32)
        totals = lax.fori_loop(0, picks, one_pick, (zero, zero, zero))
        out_ref[block] = jnp.concatenate(
            [jnp.sum(total, axis=0, keepdims=True) for total in totals], axis=0
        )
        return carry

    lax.fori_loop(0, blocks, one_block, 0)


def pair_forces(extended, neighbor_blocks):
    coords, span, lanes = extended.shape
    blocks, picks = neighbor_blocks.shape
    rows = jnp.transpose(extended, (1, 0, 2))
    cols = jnp.broadcast_to(rows[:, :, :, None], (span, coords, lanes, lanes))
    pairs = blocks * picks * lanes * lanes
    out = pl.pallas_call(
        force_kernel,
        out_shape=jax.ShapeDtypeStruct((blocks, 3, lanes), jnp.float32),
        in_specs=[
            pl.BlockSpec(memory_space=pltpu.SMEM),
            pl.BlockSpec(memory_space=pltpu.VMEM),
            pl.BlockSpec(memory_space=pltpu.VMEM),
        ],
        out_specs=pl.BlockSpec(memory_space=pltpu.VMEM),
        cost_estimate=pl.CostEstimate(
            flops=26 * pairs, transcendentals=2 * pairs, bytes_accessed=4 * cols.size
        ),
    )(neighbor_blocks.reshape(-1), rows, cols)
    return jnp.transpose(out, (1, 0, 2))


def neighbours(block, axis, dim):
    count = lax.axis_size(axis)
    forward = [(i, i + 1) for i in range(count - 1)]
    backward = [(target, source) for source, target in forward]
    low = lax.ppermute(lax.slice_in_dim(block, block.shape[dim] - 1, None, axis=dim), axis, forward)
    high = lax.ppermute(lax.slice_in_dim(block, 0, 1, axis=dim), axis, backward)
    return (low, high)


def shifted(block, low, high, dim):
    size = block.shape[dim]
    up = jnp.concatenate([lax.slice_in_dim(block, 1, size, axis=dim), high], axis=dim)
    down = jnp.concatenate([low, lax.slice_in_dim(block, 0, size - 1, axis=dim)], axis=dim)
    return (up, down)


def relax_step(center):
    z_low, z_high = neighbours(center, "slab", 1)
    y_low, y_high = neighbours(center, "tile", 2)
    z_up, z_down = shifted(center, z_low, z_high, 1)
    y_up, y_down = shifted(center, y_low, y_high, 2)
    sideways = jnp.pad(center, ((0, 0), (0, 0), (0, 0), (1, 1)))
    beside_all = z_up + z_down
    beside_all = beside_all + y_up + y_down
    beside_all = beside_all + sideways[..., 2:] + sideways[..., :-2]
    spread = jnp.array(DIFFUSION, jnp.float32)[:, None, None, None]
    losses = jnp.array(DECAY, jnp.float32)[:, None, None, None]
    return center + spread * (beside_all - 6.0 * center) - losses * center


def bits_of(width):
    return max(1, (width - 1).bit_length())


def gather_windows(values, starts, length):
    channels, cells = values.shape
    width = cells + length
    rows = starts.shape[0]
    padded = jnp.pad(values, ((0, 0), (0, length)))
    held = jnp.broadcast_to(padded[:, None, :], (channels, rows, width))
    for bit in range(0, bits_of(cells), RADIX_BITS):
        digit = ((starts >> bit) & ((1 << RADIX_BITS) - 1))[None, :, None]
        moved = held
        for value in range(1, 1 << RADIX_BITS):
            moved = jnp.where(digit == value, jnp.roll(held, -(value << bit), axis=2), moved)
        held = moved
    return held[:, :, :length]


def scatter_windows(windows, starts, cells):
    channels, rows, length = windows.shape
    width = cells + length
    held = jnp.pad(windows, ((0, 0), (0, 0), (0, width - length)))
    for bit in range(0, bits_of(cells), RADIX_BITS):
        digit = ((starts >> bit) & ((1 << RADIX_BITS) - 1))[None, :, None]
        moved = held
        for value in range(1, 1 << RADIX_BITS):
            moved = jnp.where(digit == value, jnp.roll(held, value << bit, axis=2), moved)
        held = moved
    return jnp.sum(held[:, :, :cells], axis=1)


def local(
    positions, radius, uptake_rate, voxel_local, cell_counts, send_counts, neighbor_blocks, field
):
    tiles = lax.axis_size("tile")
    capacity = positions.shape[1]
    blocks = capacity // 128
    slot_size = 2 * capacity // tiles
    cell = jnp.arange(capacity, dtype=jnp.int32)
    count = cell_counts[0]
    kept = jnp.where(cell < count, radius, 0.0)
    table = jnp.concatenate([positions, kept[None]], axis=0)
    extended = with_halo(table, (("tile", 1),), HB * 128)
    extended = extended.reshape(4, blocks + 2 * HB, 128)
    forces = pair_forces(extended, neighbor_blocks).reshape(3, capacity)
    sends = send_counts[0]
    ends = jnp.cumsum(sends)
    starts = ends - sends
    ranks = jnp.arange(slot_size, dtype=jnp.int32)
    valid = ranks[None, :] < sends[:, None]
    payload = jnp.stack([voxel_local.astype(jnp.float32), uptake_rate])
    windows = gather_windows(payload, starts, slot_size)
    windows = jnp.where(valid[None], windows, 0.0)
    arrived = lax.all_to_all(windows, "tile", split_axis=1, concat_axis=1, tiled=True)
    reached = arrived[0].reshape(-1).astype(jnp.int32)
    rates = arrived[1].reshape(-1)
    species, depth, rows, columns = field.shape
    planes = depth * rows
    oxygen_rows = field[0].reshape(1, planes, columns)
    oxygen = pick_exact(oxygen_rows, reached, 2 * SLOT_BLOCK)[0]
    consume = rates * oxygen / (MICHAELIS_HALF + oxygen)
    secrete = SECRETION * rates * HYPOXIA_HALF / (HYPOXIA_HALF + oxygen)
    amounts = jnp.stack([-STEP_TIME * consume, STEP_TIME * secrete])
    added = spread_voxels(amounts, reached, planes, columns)
    state = field + added.reshape(species, depth, rows, columns)
    for step in range(ITERS):
        state = relax_step(state)
    vegf = state[1]
    z_low, z_high = neighbours(vegf, "slab", 0)
    y_low, y_high = neighbours(vegf, "tile", 1)
    z_up, z_down = shifted(vegf, z_low, z_high, 0)
    y_up, y_down = shifted(vegf, y_low, y_high, 1)
    rise_z = 0.5 * (z_up - z_down)
    rise_y = 0.5 * (y_up - y_down)
    middle = jnp.pad(vegf, ((0, 0), (0, 0), (1, 1)))
    rise_x = 0.5 * (middle[..., 2:] - middle[..., :-2])
    rises = jnp.stack([rise_z, rise_y, rise_x]).reshape(3, planes, columns)
    slopes = pick_voxels(rises, reached).reshape(3, tiles, slot_size)
    returned = lax.all_to_all(slopes, "tile", split_axis=1, concat_axis=1, tiled=True)
    returned = jnp.where(valid[None], returned, 0.0)
    slope = scatter_windows(returned, starts, capacity)
    velocity = FORCE_SCALE * forces + CHEMOTAXIS * slope
    return (velocity, state)


def solution(mesh):
    placed = (
        P(None, ("slab", "tile")),
        P(("slab", "tile")),
        P(("slab", "tile")),
        P(("slab", "tile")),
        P(("slab", "tile")),
        P(("slab", "tile"), None),
        P(("slab", "tile"), None),
        P(None, "slab", "tile", None),
    )
    return jax.shard_map(
        local,
        mesh=mesh,
        in_specs=placed,
        out_specs=(P(None, ("slab", "tile")), P(None, "slab", "tile", None)),
        check_vma=False,
    )
```

```python
import jax
import jax.numpy as jnp
from jax import lax
from jax.experimental import pallas as pl
from jax.experimental.pallas import tpu as pltpu
from jax.sharding import PartitionSpec as P

HB = 4
K = 8
ITERS = 4


MICHAELIS_HALF = 0.5
HYPOXIA_HALF = 0.6
SECRETION = 0.4
STEP_TIME = 0.5
DIFFUSION = (0.16, 0.12)
DECAY = (0.0, 0.03)
REPULSION = 1.0
ADHESION = 0.35
REPEL_RANGE = 1.0
ADHERE_RANGE = 4.0
FORCE_SCALE = 0.08
CHEMOTAXIS = 1.5
SLOT_BLOCK = 512


def with_halo(block, sides, width):
    for axis, dim in sides:
        count = lax.axis_size(axis)
        forward = [(i, i + 1) for i in range(count - 1)]
        backward = [(target, source) for source, target in forward]
        low = lax.ppermute(
            lax.slice_in_dim(block, block.shape[dim] - width, None, axis=dim), axis, forward
        )
        high = lax.ppermute(lax.slice_in_dim(block, 0, width, axis=dim), axis, backward)
        block = jnp.concatenate([low, block, high], axis=dim)
    return block


def block_force(mine, others):
    offset = mine[:3, :, :, None, None] - others[:3, :, None, :, :]
    distance = jnp.sum(offset * offset, axis=0)
    strength = REPULSION * jnp.exp(-distance / REPEL_RANGE) - ADHESION * jnp.exp(
        -distance / ADHERE_RANGE
    )
    weight = mine[3][:, :, None, None] * others[3][:, None, :, :] * strength
    return jnp.sum(offset * weight[None], axis=(3, 4))


def relax(padded):
    center = padded[:, 1:-1, 1:-1]
    sideways = jnp.pad(center, ((0, 0), (0, 0), (0, 0), (1, 1)))
    beside_all = padded[:, 2:, 1:-1] + padded[:, :-2, 1:-1]
    beside_all = beside_all + padded[:, 1:-1, 2:] + padded[:, 1:-1, :-2]
    beside_all = beside_all + sideways[..., 2:] + sideways[..., :-2]
    spread = jnp.array(DIFFUSION, jnp.float32)[:, None, None, None]
    losses = jnp.array(DECAY, jnp.float32)[:, None, None, None]
    return center + spread * (beside_all - 6.0 * center) - losses * center


def routing(sends, length):
    ends = jnp.cumsum(sends)
    starts = ends - sends
    cell = jnp.arange(length, dtype=jnp.int32)
    target = jnp.sum((ends[:, None] <= cell[None, :]).astype(jnp.int32), axis=0)
    routed = target < sends.shape[0]
    target = jnp.minimum(target, sends.shape[0] - 1)
    lanes = jnp.arange(sends.shape[0], dtype=jnp.int32)
    first = jnp.sum(jnp.where(lanes[:, None] == target[None, :], starts[:, None], 0), axis=0)
    return (target, cell - first, routed)


def hot_tables(piece, planes, columns, kind=jnp.float32):
    row_hot = (piece[:, None] // columns == jnp.arange(planes, dtype=jnp.int32)[None, :]).astype(
        kind
    )
    column_hot = (piece[:, None] % columns == jnp.arange(columns, dtype=jnp.int32)[None, :]).astype(
        kind
    )
    return (row_hot, column_hot)


def split_three(values):
    high = lax.reduce_precision(values, exponent_bits=8, mantissa_bits=7)
    rest = values - high
    middle = lax.reduce_precision(rest, exponent_bits=8, mantissa_bits=7)
    return jnp.stack([high, middle, rest - middle]).astype(jnp.bfloat16)


def pick_exact(fields, reached, block):
    species, planes, columns = fields.shape
    parts = split_three(fields)
    pieces = reached.reshape(-1, block)

    def one_piece(piece):
        row_hot, column_hot = hot_tables(piece, planes, columns, jnp.bfloat16)
        picked = jnp.einsum(
            "psrx,mx->psrm", parts, column_hot, preferred_element_type=jnp.float32
        )
        picked = picked[0] + picked[1] + picked[2]
        return jnp.sum(picked * jnp.transpose(row_hot).astype(jnp.float32)[None], axis=1)

    found = lax.map(one_piece, pieces)
    return jnp.moveaxis(found, 1, 0).reshape(species, -1)


def pick_voxels(fields, reached):
    species, planes, columns = fields.shape
    pieces = reached.reshape(-1, SLOT_BLOCK)

    def one_piece(piece):
        row_hot, column_hot = hot_tables(piece, planes, columns)
        picked = jnp.einsum("srx,mx->srm", fields, column_hot, precision=lax.Precision.HIGHEST)
        return jnp.sum(picked * jnp.transpose(row_hot)[None], axis=1)

    found = lax.map(one_piece, pieces)
    return jnp.moveaxis(found, 1, 0).reshape(species, -1)


def spread_voxels(amounts, reached, planes, columns):
    species = amounts.shape[0]
    pieces = reached.reshape(-1, SLOT_BLOCK)
    shares = jnp.moveaxis(amounts.reshape(species, -1, SLOT_BLOCK), 1, 0)

    def add_piece(total, item):
        piece, share = item
        row_hot, column_hot = hot_tables(piece, planes, columns)
        weighted = share[:, :, None] * row_hot[None]
        return (
            total
            + jnp.einsum("smr,mx->srx", weighted, column_hot, precision=lax.Precision.HIGHEST),
            None,
        )

    empty = jnp.zeros((species, planes, columns), jnp.float32)
    total, unused = lax.scan(add_piece, empty, (pieces, shares))
    return total


def force_kernel(chosen_ref, rows_ref, cols_ref, out_ref):
    blocks = out_ref.shape[0]
    picks = chosen_ref.shape[0] // blocks
    chunks = cols_ref.shape[2] // 8
    shape = (8, cols_ref.shape[3])

    def one_block(block, carry):
        own = rows_ref[block + HB]
        mine = [jnp.broadcast_to(own[axis:axis + 1, :], shape) for axis in range(4)]

        def one_pick(pick, totals):
            other = chosen_ref[block * picks + pick]
            totals = list(totals)
            for chunk in range(chunks):
                part = pl.ds(chunk * 8, 8)
                offset = [mine[axis] - cols_ref[other, axis, part, :] for axis in range(3)]
                distance = offset[0] * offset[0] + offset[1] * offset[1] + offset[2] * offset[2]
                strength = REPULSION * jnp.exp(-distance / REPEL_RANGE) - ADHESION * jnp.exp(
                    -distance / ADHERE_RANGE
                )
                weight = cols_ref[other, 3, part, :] * strength
                for axis in range(3):
                    totals[axis] = totals[axis] + offset[axis] * weight
            return tuple(totals)

        zero = jnp.zeros(shape, jnp.float32)
        totals = lax.fori_loop(0, picks, one_pick, (zero, zero, zero))
        out_ref[block] = jnp.concatenate(
            [own[3:4, :] * jnp.sum(total, axis=0, keepdims=True) for total in totals], axis=0
        )
        return carry

    lax.fori_loop(0, blocks, one_block, 0)


def pair_forces(extended, neighbor_blocks):
    coords, span, lanes = extended.shape
    blocks, picks = neighbor_blocks.shape
    rows = jnp.transpose(extended, (1, 0, 2))
    cols = jnp.broadcast_to(rows[:, :, :, None], (span, coords, lanes, lanes))
    pairs = blocks * picks * lanes * lanes
    out = pl.pallas_call(
        force_kernel,
        out_shape=jax.ShapeDtypeStruct((blocks, 3, lanes), jnp.float32),
        in_specs=[
            pl.BlockSpec(memory_space=pltpu.SMEM),
            pl.BlockSpec(memory_space=pltpu.VMEM),
            pl.BlockSpec(memory_space=pltpu.VMEM),
        ],
        out_specs=pl.BlockSpec(memory_space=pltpu.VMEM),
        cost_estimate=pl.CostEstimate(
            flops=26 * pairs, transcendentals=2 * pairs, bytes_accessed=4 * cols.size
        ),
    )(neighbor_blocks.reshape(-1), rows, cols)
    return jnp.transpose(out, (1, 0, 2))


def neighbours(block, axis, dim):
    count = lax.axis_size(axis)
    forward = [(i, i + 1) for i in range(count - 1)]
    backward = [(target, source) for source, target in forward]
    low = lax.ppermute(lax.slice_in_dim(block, block.shape[dim] - 1, None, axis=dim), axis, forward)
    high = lax.ppermute(lax.slice_in_dim(block, 0, 1, axis=dim), axis, backward)
    return (low, high)


def shifted(block, low, high, dim):
    size = block.shape[dim]
    up = jnp.concatenate([lax.slice_in_dim(block, 1, size, axis=dim), high], axis=dim)
    down = jnp.concatenate([low, lax.slice_in_dim(block, 0, size - 1, axis=dim)], axis=dim)
    return (up, down)


def relax_step(center):
    z_low, z_high = neighbours(center, "slab", 1)
    y_low, y_high = neighbours(center, "tile", 2)
    z_up, z_down = shifted(center, z_low, z_high, 1)
    y_up, y_down = shifted(center, y_low, y_high, 2)
    sideways = jnp.pad(center, ((0, 0), (0, 0), (0, 0), (1, 1)))
    beside_all = z_up + z_down
    beside_all = beside_all + y_up + y_down
    beside_all = beside_all + sideways[..., 2:] + sideways[..., :-2]
    spread = jnp.array(DIFFUSION, jnp.float32)[:, None, None, None]
    losses = jnp.array(DECAY, jnp.float32)[:, None, None, None]
    return center + spread * (beside_all - 6.0 * center) - losses * center


def bits_of(width):
    return max(1, (width - 1).bit_length())


def gather_windows(values, starts, length):
    channels, cells = values.shape
    width = cells + length
    rows = starts.shape[0]
    padded = jnp.pad(values, ((0, 0), (0, length)))
    held = jnp.broadcast_to(padded[:, None, :], (channels, rows, width))
    for bit in range(bits_of(cells)):
        step = 1 << bit
        take = ((starts >> bit) & 1 == 1)[None, :, None]
        held = jnp.where(take, jnp.roll(held, -step, axis=2), held)
    return held[:, :, :length]


def scatter_windows(windows, starts, cells):
    channels, rows, length = windows.shape
    width = cells + length
    held = jnp.pad(windows, ((0, 0), (0, 0), (0, width - length)))
    for bit in range(bits_of(cells)):
        step = 1 << bit
        take = ((starts >> bit) & 1 == 1)[None, :, None]
        held = jnp.where(take, jnp.roll(held, step, axis=2), held)
    return jnp.sum(held[:, :, :cells], axis=1)


def local(
    positions, radius, uptake_rate, voxel_local, cell_counts, send_counts, neighbor_blocks, field
):
    tiles = lax.axis_size("tile")
    capacity = positions.shape[1]
    blocks = capacity // 128
    slot_size = 2 * capacity // tiles
    cell = jnp.arange(capacity, dtype=jnp.int32)
    count = cell_counts[0]
    kept = jnp.where(cell < count, radius, 0.0)
    table = jnp.concatenate([positions, kept[None]], axis=0)
    extended = with_halo(table, (("tile", 1),), HB * 128)
    extended = extended.reshape(4, blocks + 2 * HB, 128)
    forces = pair_forces(extended, neighbor_blocks).reshape(3, capacity)
    sends = send_counts[0]
    ends = jnp.cumsum(sends)
    starts = ends - sends
    ranks = jnp.arange(slot_size, dtype=jnp.int32)
    valid = ranks[None, :] < sends[:, None]
    payload = jnp.stack([voxel_local.astype(jnp.float32), uptake_rate])
    windows = gather_windows(payload, starts, slot_size)
    windows = jnp.where(valid[None], windows, 0.0)
    arrived = lax.all_to_all(windows, "tile", split_axis=1, concat_axis=1, tiled=True)
    reached = arrived[0].reshape(-1).astype(jnp.int32)
    rates = arrived[1].reshape(-1)
    species, depth, rows, columns = field.shape
    planes = depth * rows
    oxygen_rows = field[0].reshape(1, planes, columns)
    oxygen = pick_exact(oxygen_rows, reached, 2 * SLOT_BLOCK)[0]
    consume = rates * oxygen / (MICHAELIS_HALF + oxygen)
    secrete = SECRETION * rates * HYPOXIA_HALF / (HYPOXIA_HALF + oxygen)
    amounts = jnp.stack([-STEP_TIME * consume, STEP_TIME * secrete])
    added = spread_voxels(amounts, reached, planes, columns)
    state = field + added.reshape(species, depth, rows, columns)
    for step in range(ITERS):
        state = relax_step(state)
    vegf = state[1]
    z_low, z_high = neighbours(vegf, "slab", 0)
    y_low, y_high = neighbours(vegf, "tile", 1)
    z_up, z_down = shifted(vegf, z_low, z_high, 0)
    y_up, y_down = shifted(vegf, y_low, y_high, 1)
    rise_z = 0.5 * (z_up - z_down)
    rise_y = 0.5 * (y_up - y_down)
    middle = jnp.pad(vegf, ((0, 0), (0, 0), (1, 1)))
    rise_x = 0.5 * (middle[..., 2:] - middle[..., :-2])
    rises = jnp.stack([rise_z, rise_y, rise_x]).reshape(3, planes, columns)
    slopes = pick_voxels(rises, reached).reshape(3, tiles, slot_size)
    returned = lax.all_to_all(slopes, "tile", split_axis=1, concat_axis=1, tiled=True)
    returned = jnp.where(valid[None], returned, 0.0)
    slope = scatter_windows(returned, starts, capacity)
    velocity = FORCE_SCALE * forces + CHEMOTAXIS * slope
    return (velocity, state)


def solution(mesh):
    placed = (
        P(None, ("slab", "tile")),
        P(("slab", "tile")),
        P(("slab", "tile")),
        P(("slab", "tile")),
        P(("slab", "tile")),
        P(("slab", "tile"), None),
        P(("slab", "tile"), None),
        P(None, "slab", "tile", None),
    )
    return jax.shard_map(
        local,
        mesh=mesh,
        in_specs=placed,
        out_specs=(P(None, ("slab", "tile")), P(None, "slab", "tile", None)),
        check_vma=False,
    )
```
